256 devices in a mesh: shard: 32 (over z, x), tensor: 4 (over y), section: 2 (over core).
Axes of the slice: x: 4, y: 4, z: 8, core: 2. Of those that a mesh axis runs over, the one named last changes fastest.
Arguments:
- gradient: bfloat16 [32, 512, 2048], P(('tensor', 'section'), 'shard'), may hold values from -48 to 48
- momentum: float32 [32, 512, 2048], P(('tensor', 'section'), 'shard'), may hold values from -8 to 8
- normed: bfloat16 [32768, 512], P(('shard', 'section'), 'tensor'), may hold values from -6 to 6
- ln_gain: float32 [512], P('tensor'), may hold values from 0.5 to 1.5
- ln_bias: float32 [512], P('tensor'), may hold values from -3 to 3
- ln_cotangent: bfloat16 [32768, 512], P(('shard', 'section'), 'tensor'), may hold values from -0.125 to 0.125
- router_cotangent: bfloat16 [32768, 32], P(('shard', 'section')), may hold values from -0.125 to 0.125
- first_moment: float32 [34, 512], P(None, 'tensor'), may hold values from -3 to 3
- second_moment: float32 [34, 512], P(None, 'tensor'), may hold values from 0.5 to 5
Outputs:
- next_momentum: float32 [32, 512, 2048], P(('tensor', 'section'), 'shard')
- update: float32 [32, 512, 2048], P(('tensor', 'section'), 'shard')
- next_first: float32 [34, 512], P(None, 'tensor')
- next_second: float32 [34, 512], P(None, 'tensor')
- adam_step: float32 [34, 512], P(None, 'tensor')
The draws below stay inside these ranges and needn't reach their ends.
All inputs are finite; a program needn't handle non-finite values.
Results may differ from the reference program's by a relative error of at most 0.035.
Values may be sent and summed in bfloat16 or wider, within the bound.
No kernel may reach another device: no remote copies, remote signals or barrier semaphores. Data moves between devices by JAX's collectives and lax.ppermute only.
A program may use at most 64 MiB of HBM per device.

```python
import math
import jax
import jax.numpy as jnp
from jax import lax

D = 512
FF = 2048
EXPERTS = 32
ITERS = 5
MATS = 32
TOKENS = 32768
VECS = 34


def draw_gradient(key, part):
    keys = jax.random.split(key, 3)
    shape = (MATS, D, FF)
    base = jnp.clip(jax.random.normal(keys[0], shape, jnp.float32), -4.0, 4.0)
    row_scale = jnp.exp(jax.random.uniform(keys[1], (MATS, D, 1), jnp.float32, math.log(0.3), math.log(3.0)))
    col_scale = jnp.exp(jax.random.uniform(keys[2], (MATS, 1, FF), jnp.float32, math.log(0.3), math.log(3.0)))
    value = base * row_scale * col_scale
    return value.astype(jnp.bfloat16)


def block_levels(key, extent, pieces, low, largest):
    level, own = 1.0, jax.random.fold_in(key, 6)
    for axis_at, shards_of in pieces:
        steps = jnp.exp(jax.random.uniform(jax.random.fold_in(own, axis_at), (shards_of,), jnp.float32, low / len(pieces), largest / len(pieces)))
        level = level * jnp.repeat(steps, extent[axis_at] // shards_of).reshape([-1 if axis == axis_at else 1 for axis in range(len(extent))])
    return level


def noise(rng, shape, scale, reach, shards=(), held_as=jnp.bfloat16):
    array = scale * jax.random.normal(rng, shape, jnp.float32)
    if shards:
        array = array * block_levels(rng, shape, shards, -0.22, 0.18)
    return jnp.clip(array, -reach, reach).astype(held_as)


def setup_inputs(seed: int = 0) -> dict:
    key_list = jax.random.split(jax.random.key(seed), 10)
    return {
        "gradient": draw_gradient(jax.random.fold_in(key_list[9], 71), 0),
        "momentum": noise(key_list[1], (MATS, D, FF), 2.0, 8.0, ((0, 8), (1, 32)), jnp.float32),
        "normed": noise(key_list[2], (TOKENS, D), 1.0, 6.0, ((0, 64), (1, 4))),
        "ln_gain": jnp.clip(1.0 + 0.1 * jax.random.normal(key_list[3], (D,), jnp.float32), 0.5, 1.5),
        "ln_bias": noise(key_list[4], (D,), 0.5, 3.0, ((0, 4),), jnp.float32),
        "ln_cotangent": noise(key_list[5], (TOKENS, D), (TOKENS // 16) ** -0.5, 0.125, ((0, 64), (1, 4))),
        "router_cotangent": noise(key_list[6], (TOKENS, EXPERTS), (TOKENS // 16) ** -0.5, 0.125, ((0, 64),)),
        "first_moment": noise(key_list[7], (VECS, D), 0.5, 3.0, ((1, 4),), jnp.float32),
        "second_moment": jnp.clip(jnp.exp(math.log(5.0) - 2.3025851 * jax.random.uniform(key_list[8], (VECS, D), jnp.float32) ** block_levels(key_list[8], (VECS, D), ((1, 4),), -0.2, 0.2)), 0.5, 5.0),
    }


MUON_DECAY = 0.95
LINEAR_TERM = 3.4445
CUBIC_TERM = -4.775
QUINTIC_TERM = 2.0315
NORM_EPSILON = 1e-07
ADAM_FIRST = 0.9
ADAM_SECOND = 0.95
ADAM_EPSILON = 1e-08

def orthogonalize(matrix):
    wide = matrix.astype(jnp.float32)
    total = jnp.sqrt(jnp.sum(wide * wide))
    iterate = (wide / (total + NORM_EPSILON)).astype(jnp.bfloat16)
    for repeat in range(ITERS):
        gram = jnp.dot(iterate, iterate.T, preferred_element_type=jnp.float32)
        gram_half = gram.astype(jnp.bfloat16)
        poly = (CUBIC_TERM * gram + QUINTIC_TERM * jnp.dot(gram_half, gram_half, preferred_element_type=jnp.float32)).astype(jnp.bfloat16)
        iterate = (LINEAR_TERM * iterate.astype(jnp.float32) + jnp.dot(poly, iterate, preferred_element_type=jnp.float32)).astype(jnp.bfloat16)
    return iterate.astype(jnp.float32) * math.sqrt(FF)

def reference(gradient, momentum, normed, ln_gain, ln_bias, ln_cotangent, router_cotangent, first_moment, second_moment):
    grad_float = gradient.astype(jnp.float32)
    next_momentum = MUON_DECAY * momentum + grad_float
    nesterov = (grad_float + MUON_DECAY * next_momentum).astype(jnp.bfloat16)
    update = lax.map(orthogonalize, nesterov)
    normed_float = normed.astype(jnp.float32)
    cot_float = ln_cotangent.astype(jnp.float32)
    ln_out = (ln_gain[None, :] * normed_float + ln_bias[None, :]).astype(jnp.bfloat16)
    gain_grad = lax.optimization_barrier(jnp.sum(cot_float * normed_float, axis=0))
    bias_grad = lax.optimization_barrier(jnp.sum(cot_float, axis=0))
    router_grad = jnp.dot(router_cotangent.T, ln_out, preferred_element_type=jnp.float32)
    vec_grad = jnp.concatenate([gain_grad[None, :], bias_grad[None, :], router_grad], axis=0)
    next_first = ADAM_FIRST * first_moment + (1.0 - ADAM_FIRST) * vec_grad
    next_second = ADAM_SECOND * second_moment + (1.0 - ADAM_SECOND) * vec_grad * vec_grad
    adam_step = next_first / (jnp.sqrt(next_second) + ADAM_EPSILON)
    return (next_momentum, update, next_first, next_second, adam_step)
```

```python
import math

import jax
import jax.numpy as jnp
import numpy as np
from jax import lax
from jax.sharding import Mesh
from jax.sharding import PartitionSpec as P

FF = 2048
ITERS = 5


MUON_DECAY = 0.95
LINEAR_TERM = 3.4445
CUBIC_TERM = -4.775
QUINTIC_TERM = 2.0315
NORM_EPSILON = 1e-07
ADAM_FIRST = 0.9
ADAM_SECOND = 0.95
ADAM_EPSILON = 1e-08

SHARD = ("outer", "inner")


def orthogonalize(blocks):
    squares = jnp.sum(jnp.square(blocks.astype(jnp.float32)), axis=(1, 2))
    total = jnp.sqrt(squares)
    iterate = (blocks.astype(jnp.float32) / (total + NORM_EPSILON)[:, None, None]).astype(
        jnp.bfloat16
    )
    for repeat in range(ITERS):
        gram = jnp.einsum("kij,klj->kil", iterate, iterate, preferred_element_type=jnp.float32)
        gram_half = gram.astype(jnp.bfloat16)
        square_term = jnp.einsum(
            "kij,kjl->kil", gram_half, gram_half, preferred_element_type=jnp.float32
        )
        poly = (CUBIC_TERM * gram + QUINTIC_TERM * square_term).astype(jnp.bfloat16)
        product = jnp.einsum("kij,kjl->kil", poly, iterate, preferred_element_type=jnp.float32)
        iterate = (LINEAR_TERM * iterate.astype(jnp.float32) + product).astype(jnp.bfloat16)
    return iterate


def vector_step(normed, ln_gain, ln_bias, ln_cotangent, router_cotangent, first_moment, second_moment):
    normed_float = normed.astype(jnp.float32)
    cot_float = ln_cotangent.astype(jnp.float32)
    ln_out = (ln_gain[None, :] * normed_float + ln_bias[None, :]).astype(jnp.bfloat16)
    gain_local = jnp.sum(cot_float * normed_float, axis=0)
    bias_local = jnp.sum(cot_float, axis=0)
    router_local = lax.dot_general(
        router_cotangent, ln_out, (((0,), (0,)), ((), ())), preferred_element_type=jnp.float32
    )
    local = jnp.concatenate([gain_local[None, :], bias_local[None, :], router_local], axis=0)
    vec_grad = lax.psum(local, SHARD + ("section",))
    next_first = ADAM_FIRST * first_moment + (1.0 - ADAM_FIRST) * vec_grad
    next_second = ADAM_SECOND * second_moment + (1.0 - ADAM_SECOND) * vec_grad * vec_grad
    adam_step = next_first / (jnp.sqrt(next_second) + ADAM_EPSILON)
    return next_first, next_second, adam_step


def on_device(
    gradient,
    momentum,
    normed,
    ln_gain,
    ln_bias,
    ln_cotangent,
    router_cotangent,
    first_moment,
    second_moment,
):
    next_first, next_second, adam_step = vector_step(
        normed, ln_gain, ln_bias, ln_cotangent, router_cotangent, first_moment, second_moment
    )
    grad_float = gradient.astype(jnp.float32)
    next_momentum = MUON_DECAY * momentum + grad_float
    nesterov = (grad_float + MUON_DECAY * next_momentum).astype(jnp.bfloat16)
    nesterov, next_first, next_second, adam_step = lax.optimization_barrier(
        (nesterov, next_first, next_second, adam_step)
    )
    count_all, rows_piece, cols_full = nesterov.shape
    inner = lax.axis_size("inner")
    outer = lax.axis_size("outer")
    slots = -(-count_all // inner)
    padded = jnp.pad(nesterov, ((0, slots * inner - count_all), (0, 0), (0, 0)))
    strip = lax.all_to_all(padded, "inner", split_axis=0, concat_axis=1, tiled=True)
    blocks = lax.all_gather(strip, "outer", axis=1, tiled=True)
    result = orthogonalize(blocks)
    strip_rows = inner * rows_piece
    mine = lax.dynamic_slice_in_dim(result, lax.axis_index("outer") * strip_rows, strip_rows, axis=1)
    outgoing = mine.reshape(slots, inner, rows_piece, cols_full).transpose(1, 0, 2, 3)
    returned = lax.all_to_all(outgoing, "inner", split_axis=0, concat_axis=0, tiled=True)
    ordered = returned.reshape(slots * inner, rows_piece, cols_full)
    update = ordered[:count_all].astype(jnp.float32) * math.sqrt(FF)
    return (next_momentum, update, next_first, next_second, adam_step)


def inner_size(mesh):
    row = np.asarray(mesh.devices)[:, 0, 0]
    try:
        size = len({tuple(device.coords)[0] for device in row})
    except (AttributeError, TypeError):
        size = 0
    if size <= 1 or row.size % size:
        size = math.gcd(row.size, 4)
    return size


def solution(mesh):
    devices = np.asarray(mesh.devices)
    shard, tensor, section = devices.shape
    inner = inner_size(mesh)
    split = Mesh(
        devices.reshape(shard // inner, inner, tensor, section),
        ("outer", "inner", "tensor", "section"),
    )
    return jax.shard_map(
        on_device,
        mesh=split,
        in_specs=(
            P(("tensor", "section"), SHARD, None),
            P(("tensor", "section"), SHARD, None),
            P((*SHARD, "section"), "tensor"),
            P("tensor"),
            P("tensor"),
            P((*SHARD, "section"), "tensor"),
            P((*SHARD, "section"), None),
            P(None, "tensor"),
            P(None, "tensor"),
        ),
        out_specs=(
            P(("tensor", "section"), SHARD, None),
            P(("tensor", "section"), SHARD, None),
            P(None, "tensor"),
            P(None, "tensor"),
            P(None, "tensor"),
        ),
        check_vma=False,
    )
```

```python
import math

import jax
import jax.numpy as jnp
import numpy as np
from jax import lax
from jax.sharding import Mesh
from jax.sharding import PartitionSpec as P

FF = 2048
ITERS = 5


MUON_DECAY = 0.95
LINEAR_TERM = 3.4445
CUBIC_TERM = -4.775
QUINTIC_TERM = 2.0315
NORM_EPSILON = 1e-07
ADAM_FIRST = 0.9
ADAM_SECOND = 0.95
ADAM_EPSILON = 1e-08

SHARD = ("outer", "inner")


def orthogonalize(blocks):
    squares = jnp.sum(jnp.square(blocks.astype(jnp.float32)), axis=(1, 2))
    total = jnp.sqrt(squares)
    iterate = (blocks.astype(jnp.float32) / (total + NORM_EPSILON)[:, None, None]).astype(
        jnp.bfloat16
    )
    for repeat in range(ITERS):
        gram = jnp.einsum("kij,klj->kil", iterate, iterate, preferred_element_type=jnp.float32)
        gram_half = gram.astype(jnp.bfloat16)
        square_term = jnp.einsum(
            "kij,kjl->kil", gram_half, gram_half, preferred_element_type=jnp.float32
        )
        poly = (CUBIC_TERM * gram + QUINTIC_TERM * square_term).astype(jnp.bfloat16)
        product = jnp.einsum("kij,kjl->kil", poly, iterate, preferred_element_type=jnp.float32)
        iterate = (LINEAR_TERM * iterate.astype(jnp.float32) + product).astype(jnp.bfloat16)
    return iterate


def vector_step(
    normed, ln_gain, ln_bias, ln_cotangent, router_cotangent, first_moment, second_moment, after
):
    normed_float = normed.astype(jnp.float32)
    cot_float = ln_cotangent.astype(jnp.float32)
    ln_out = (ln_gain[None, :] * normed_float + ln_bias[None, :]).astype(jnp.bfloat16)
    gain_local = jnp.sum(cot_float * normed_float, axis=0)
    bias_local = jnp.sum(cot_float, axis=0)
    router_local = lax.dot_general(
        router_cotangent, ln_out, (((0,), (0,)), ((), ())), preferred_element_type=jnp.float32
    )
    local = jnp.concatenate([gain_local[None, :], bias_local[None, :], router_local], axis=0)
    local, after = lax.optimization_barrier((local, after))
    everyone = lax.all_gather(local, SHARD + ("section",), axis=0, tiled=False)
    vec_grad = jnp.sum(everyone, axis=0)
    next_first = ADAM_FIRST * first_moment + (1.0 - ADAM_FIRST) * vec_grad
    next_second = ADAM_SECOND * second_moment + (1.0 - ADAM_SECOND) * vec_grad * vec_grad
    adam_step = next_first / (jnp.sqrt(next_second) + ADAM_EPSILON)
    return next_first, next_second, adam_step


def on_device(
    gradient,
    momentum,
    normed,
    ln_gain,
    ln_bias,
    ln_cotangent,
    router_cotangent,
    first_moment,
    second_moment,
):
    grad_float = gradient.astype(jnp.float32)
    next_momentum = MUON_DECAY * momentum + grad_float
    nesterov = (grad_float + MUON_DECAY * next_momentum).astype(jnp.bfloat16)
    count_all, rows_piece, cols_full = nesterov.shape
    inner = lax.axis_size("inner")
    outer = lax.axis_size("outer")
    slots = -(-count_all // inner)
    padded = jnp.pad(nesterov, ((0, slots * inner - count_all), (0, 0), (0, 0)))
    strip = lax.all_to_all(padded, "inner", split_axis=0, concat_axis=1, tiled=True)
    blocks = lax.all_gather(strip, "outer", axis=1, tiled=True)
    next_first, next_second, adam_step = vector_step(
        normed, ln_gain, ln_bias, ln_cotangent, router_cotangent, first_moment, second_moment, blocks
    )
    result = orthogonalize(blocks)
    strip_rows = inner * rows_piece
    mine = lax.dynamic_slice_in_dim(result, lax.axis_index("outer") * strip_rows, strip_rows, axis=1)
    outgoing = mine.reshape(slots, inner, rows_piece, cols_full).transpose(1, 0, 2, 3)
    returned = lax.all_to_all(outgoing, "inner", split_axis=0, concat_axis=0, tiled=True)
    ordered = returned.reshape(slots * inner, rows_piece, cols_full)
    update = ordered[:count_all].astype(jnp.float32) * math.sqrt(FF)
    return (next_momentum, update, next_first, next_second, adam_step)


def inner_size(mesh):
    row = np.asarray(mesh.devices)[:, 0, 0]
    try:
        size = len({tuple(device.coords)[0] for device in row})
    except (AttributeError, TypeError):
        size = 0
    if size <= 1 or row.size % size:
        size = math.gcd(row.size, 4)
    return size


def solution(mesh):
    devices = np.asarray(mesh.devices)
    shard, tensor, section = devices.shape
    inner = inner_size(mesh)
    split = Mesh(
        devices.reshape(shard // inner, inner, tensor, section),
        ("outer", "inner", "tensor", "section"),
    )
    return jax.shard_map(
        on_device,
        mesh=split,
        in_specs=(
            P(("tensor", "section"), SHARD, None),
            P(("tensor", "section"), SHARD, None),
            P((*SHARD, "section"), "tensor"),
            P("tensor"),
            P("tensor"),
            P((*SHARD, "section"), "tensor"),
            P((*SHARD, "section"), None),
            P(None, "tensor"),
            P(None, "tensor"),
        ),
        out_specs=(
            P(("tensor", "section"), SHARD, None),
            P(("tensor", "section"), SHARD, None),
            P(None, "tensor"),
            P(None, "tensor"),
            P(None, "tensor"),
        ),
        check_vma=False,
    )
```

```python
import math

import jax
import jax.numpy as jnp
import numpy as np
from jax import lax
from jax.sharding import Mesh
from jax.sharding import PartitionSpec as P

FF = 2048
ITERS = 5


MUON_DECAY = 0.95
LINEAR_TERM = 3.4445
CUBIC_TERM = -4.775
QUINTIC_TERM = 2.0315
NORM_EPSILON = 1e-07
ADAM_FIRST = 0.9
ADAM_SECOND = 0.95
ADAM_EPSILON = 1e-08

SHARD = ("outer", "inner")


def orthogonalize(blocks):
    squares = jnp.sum(jnp.square(blocks.astype(jnp.float32)), axis=(1, 2))
    total = jnp.sqrt(squares)
    iterate = (blocks.astype(jnp.float32) / (total + NORM_EPSILON)[:, None, None]).astype(
        jnp.bfloat16
    )
    for repeat in range(ITERS):
        gram = jnp.einsum("kij,klj->kil", iterate, iterate, preferred_element_type=jnp.float32)
        gram_half = gram.astype(jnp.bfloat16)
        square_term = jnp.einsum(
            "kij,kjl->kil", gram_half, gram_half, preferred_element_type=jnp.float32
        )
        poly = (CUBIC_TERM * gram + QUINTIC_TERM * square_term).astype(jnp.bfloat16)
        product = jnp.einsum("kij,kjl->kil", poly, iterate, preferred_element_type=jnp.float32)
        iterate = (LINEAR_TERM * iterate.astype(jnp.float32) + product).astype(jnp.bfloat16)
    return iterate


def butterfly_sum(value, axis):
    size = lax.axis_size(axis)
    if size & (size - 1):
        return jnp.sum(lax.all_gather(value, axis, axis=0, tiled=False), axis=0)
    step = 1
    while step < size:
        partner = lax.ppermute(value, axis, [(i, i ^ step) for i in range(size)])
        value = value + partner
        step *= 2
    return value


def vector_step(normed, ln_gain, ln_bias, ln_cotangent, router_cotangent, first_moment, second_moment):
    normed_float = normed.astype(jnp.float32)
    cot_float = ln_cotangent.astype(jnp.float32)
    ln_out = (ln_gain[None, :] * normed_float + ln_bias[None, :]).astype(jnp.bfloat16)
    gain_local = jnp.sum(cot_float * normed_float, axis=0)
    bias_local = jnp.sum(cot_float, axis=0)
    router_local = lax.dot_general(
        router_cotangent, ln_out, (((0,), (0,)), ((), ())), preferred_element_type=jnp.float32
    )
    local = jnp.concatenate([gain_local[None, :], bias_local[None, :], router_local], axis=0)
    vec_grad = local
    for axis in ("section",) + SHARD:
        vec_grad = butterfly_sum(vec_grad, axis)
    next_first = ADAM_FIRST * first_moment + (1.0 - ADAM_FIRST) * vec_grad
    next_second = ADAM_SECOND * second_moment + (1.0 - ADAM_SECOND) * vec_grad * vec_grad
    adam_step = next_first / (jnp.sqrt(next_second) + ADAM_EPSILON)
    return next_first, next_second, adam_step


def on_device(
    gradient,
    momentum,
    normed,
    ln_gain,
    ln_bias,
    ln_cotangent,
    router_cotangent,
    first_moment,
    second_moment,
):
    grad_float = gradient.astype(jnp.float32)
    next_momentum = MUON_DECAY * momentum + grad_float
    nesterov = (grad_float + MUON_DECAY * next_momentum).astype(jnp.bfloat16)
    count_all, rows_piece, cols_full = nesterov.shape
    inner = lax.axis_size("inner")
    outer = lax.axis_size("outer")
    slots = -(-count_all // inner)
    padded = jnp.pad(nesterov, ((0, slots * inner - count_all), (0, 0), (0, 0)))
    strip = lax.all_to_all(padded, "inner", split_axis=0, concat_axis=1, tiled=True)
    blocks = lax.all_gather(strip, "outer", axis=1, tiled=True)
    next_first, next_second, adam_step = vector_step(
        normed, ln_gain, ln_bias, ln_cotangent, router_cotangent, first_moment, second_moment
    )
    result = orthogonalize(blocks)
    strip_rows = inner * rows_piece
    mine = lax.dynamic_slice_in_dim(result, lax.axis_index("outer") * strip_rows, strip_rows, axis=1)
    outgoing = mine.reshape(slots, inner, rows_piece, cols_full).transpose(1, 0, 2, 3)
    returned = lax.all_to_all(outgoing, "inner", split_axis=0, concat_axis=0, tiled=True)
    ordered = returned.reshape(slots * inner, rows_piece, cols_full)
    update = ordered[:count_all].astype(jnp.float32) * math.sqrt(FF)
    return (next_momentum, update, next_first, next_second, adam_step)


def inner_size(mesh):
    row = np.asarray(mesh.devices)[:, 0, 0]
    try:
        size = len({tuple(device.coords)[0] for device in row})
    except (AttributeError, TypeError):
        size = 0
    if size <= 1 or row.size % size:
        size = math.gcd(row.size, 4)
    return size


def solution(mesh):
    devices = np.asarray(mesh.devices)
    shard, tensor, section = devices.shape
    inner = inner_size(mesh)
    split = Mesh(
        devices.reshape(shard // inner, inner, tensor, section),
        ("outer", "inner", "tensor", "section"),
    )
    return jax.shard_map(
        on_device,
        mesh=split,
        in_specs=(
            P(("tensor", "section"), SHARD, None),
            P(("tensor", "section"), SHARD, None),
            P((*SHARD, "section"), "tensor"),
            P("tensor"),
            P("tensor"),
            P((*SHARD, "section"), "tensor"),
            P((*SHARD, "section"), None),
            P(None, "tensor"),
            P(None, "tensor"),
        ),
        out_specs=(
            P(("tensor", "section"), SHARD, None),
            P(("tensor", "section"), SHARD, None),
            P(None, "tensor"),
            P(None, "tensor"),
            P(None, "tensor"),
        ),
        check_vma=False,
    )
```

```python
import math

import jax
import jax.numpy as jnp
import numpy as np
from jax import lax
from jax.sharding import Mesh
from jax.sharding import PartitionSpec as P

FF = 2048
ITERS = 5


MUON_DECAY = 0.95
LINEAR_TERM = 3.4445
CUBIC_TERM = -4.775
QUINTIC_TERM = 2.0315
NORM_EPSILON = 1e-07
ADAM_FIRST = 0.9
ADAM_SECOND = 0.95
ADAM_EPSILON = 1e-08

SHARD = ("outer", "inner")


def shift(value, axis, k):
    size = lax.axis_size(axis)
    if k % size == 0:
        return value
    return lax.ppermute(value, axis, [(i, (i + k) % size) for i in range(size)])


def ring_gather(strip, axis):
    size = lax.axis_size(axis)
    cols = strip.shape[-1]
    ahead, behind = [], []
    from_behind = from_ahead = strip
    for distance in range(1, size // 2 + 1):
        if 2 * distance == size:
            half = cols // 2
            first = shift(from_behind[..., :half], axis, 1)
            second = shift(from_ahead[..., half:], axis, -1)
            ahead.append(jnp.concatenate([first, second], axis=-1))
            break
        from_behind = shift(from_behind, axis, 1)
        from_ahead = shift(from_ahead, axis, -1)
        ahead.append(from_ahead)
        behind.append(from_behind)
    return jnp.concatenate([strip] + ahead + behind[::-1], axis=1)


def orthogonalize(blocks):
    squares = jnp.sum(jnp.square(blocks.astype(jnp.float32)), axis=(1, 2))
    total = jnp.sqrt(squares)
    iterate = (blocks.astype(jnp.float32) / (total + NORM_EPSILON)[:, None, None]).astype(
        jnp.bfloat16
    )
    for repeat in range(ITERS):
        gram = jnp.einsum("kij,klj->kil", iterate, iterate, preferred_element_type=jnp.float32)
        gram_half = gram.astype(jnp.bfloat16)
        square_term = jnp.einsum(
            "kij,kjl->kil", gram_half, gram_half, preferred_element_type=jnp.float32
        )
        poly = (CUBIC_TERM * gram + QUINTIC_TERM * square_term).astype(jnp.bfloat16)
        product = jnp.einsum("kij,kjl->kil", poly, iterate, preferred_element_type=jnp.float32)
        iterate = (LINEAR_TERM * iterate.astype(jnp.float32) + product).astype(jnp.bfloat16)
    return iterate


def butterfly_sum(value, axis):
    size = lax.axis_size(axis)
    if size & (size - 1):
        return jnp.sum(lax.all_gather(value, axis, axis=0, tiled=False), axis=0)
    step = 1
    while step < size:
        partner = lax.ppermute(value, axis, [(i, i ^ step) for i in range(size)])
        value = value + partner
        step *= 2
    return value


def vector_step(normed, ln_gain, ln_bias, ln_cotangent, router_cotangent, first_moment, second_moment):
    normed_float = normed.astype(jnp.float32)
    cot_float = ln_cotangent.astype(jnp.float32)
    ln_out = (ln_gain[None, :] * normed_float + ln_bias[None, :]).astype(jnp.bfloat16)
    gain_local = jnp.sum(cot_float * normed_float, axis=0)
    bias_local = jnp.sum(cot_float, axis=0)
    router_local = lax.dot_general(
        router_cotangent, ln_out, (((0,), (0,)), ((), ())), preferred_element_type=jnp.float32
    )
    local = jnp.concatenate([gain_local[None, :], bias_local[None, :], router_local], axis=0)
    vec_grad = local
    for axis in ("section",) + SHARD:
        vec_grad = butterfly_sum(vec_grad, axis)
    next_first = ADAM_FIRST * first_moment + (1.0 - ADAM_FIRST) * vec_grad
    next_second = ADAM_SECOND * second_moment + (1.0 - ADAM_SECOND) * vec_grad * vec_grad
    adam_step = next_first / (jnp.sqrt(next_second) + ADAM_EPSILON)
    return next_first, next_second, adam_step


def on_device(
    gradient,
    momentum,
    normed,
    ln_gain,
    ln_bias,
    ln_cotangent,
    router_cotangent,
    first_moment,
    second_moment,
):
    grad_float = gradient.astype(jnp.float32)
    next_momentum = MUON_DECAY * momentum + grad_float
    nesterov = (grad_float + MUON_DECAY * next_momentum).astype(jnp.bfloat16)
    count_all, rows_piece, cols_full = nesterov.shape
    inner = lax.axis_size("inner")
    slots = -(-count_all // inner)
    padded = jnp.pad(nesterov, ((0, slots * inner - count_all), (0, 0), (0, 0)))
    by_owner = padded.reshape(inner, slots, rows_piece, cols_full)
    here = lax.axis_index("inner")
    strip = jnp.concatenate(
        [shift(lax.dynamic_index_in_dim(by_owner, (here + k) % inner, 0, keepdims=False), "inner", k)
         for k in range(inner)],
        axis=1,
    )
    blocks = ring_gather(strip, "outer")
    next_first, next_second, adam_step = vector_step(
        normed, ln_gain, ln_bias, ln_cotangent, router_cotangent, first_moment, second_moment
    )
    result = orthogonalize(blocks)
    back = jnp.stack(
        [shift(result[:, k * rows_piece:(k + 1) * rows_piece], "inner", -k) for k in range(inner)],
        axis=0,
    )
    twice = jnp.concatenate([back, back], axis=0)
    ordered = lax.dynamic_slice_in_dim(twice, (inner - here) % inner, inner, axis=0)
    ordered = ordered.reshape(inner * slots, rows_piece, cols_full)
    update = ordered[:count_all].astype(jnp.float32) * math.sqrt(FF)
    return (next_momentum, update, next_first, next_second, adam_step)


def inner_size(mesh):
    row = np.asarray(mesh.devices)[:, 0, 0]
    try:
        size = len({tuple(device.coords)[0] for device in row})
    except (AttributeError, TypeError):
        size = 0
    if size <= 1 or row.size % size:
        size = math.gcd(row.size, 4)
    return size


def solution(mesh):
    devices = np.asarray(mesh.devices)
    shard, tensor, section = devices.shape
    inner = inner_size(mesh)
    split = Mesh(
        devices.reshape(shard // inner, inner, tensor, section),
        ("outer", "inner", "tensor", "section"),
    )
    return jax.shard_map(
        on_device,
        mesh=split,
        in_specs=(
            P(("tensor", "section"), SHARD, None),
            P(("tensor", "section"), SHARD, None),
            P((*SHARD, "section"), "tensor"),
            P("tensor"),
            P("tensor"),
            P((*SHARD, "section"), "tensor"),
            P((*SHARD, "section"), None),
            P(None, "tensor"),
            P(None, "tensor"),
        ),
        out_specs=(
            P(("tensor", "section"), SHARD, None),
            P(("tensor", "section"), SHARD, None),
            P(None, "tensor"),
            P(None, "tensor"),
            P(None, "tensor"),
        ),
        check_vma=False,
    )
```

```python
import math

import jax
import jax.numpy as jnp
import numpy as np
from jax import lax
from jax.sharding import Mesh
from jax.sharding import PartitionSpec as P

FF = 2048
ITERS = 5


MUON_DECAY = 0.95
LINEAR_TERM = 3.4445
CUBIC_TERM = -4.775
QUINTIC_TERM = 2.0315
NORM_EPSILON = 1e-07
ADAM_FIRST = 0.9
ADAM_SECOND = 0.95
ADAM_EPSILON = 1e-08

SHARD = ("outer", "inner")


def shift(value, axis, k):
    size = lax.axis_size(axis)
    if k % size == 0:
        return value
    return lax.ppermute(value, axis, [(i, (i + k) % size) for i in range(size)])


def ring_gather(strip, axis):
    size = lax.axis_size(axis)
    cols = strip.shape[-1]
    ahead, behind = [], []
    from_behind = from_ahead = strip
    for distance in range(1, size // 2 + 1):
        if 2 * distance == size:
            half = cols // 2
            first = shift(from_behind[..., :half], axis, 1)
            second = shift(from_ahead[..., half:], axis, -1)
            ahead.append(jnp.concatenate([first, second], axis=-1))
            break
        from_behind = shift(from_behind, axis, 1)
        from_ahead = shift(from_ahead, axis, -1)
        ahead.append(from_ahead)
        behind.append(from_behind)
    return jnp.concatenate([strip] + ahead + behind[::-1], axis=1)


def orthogonalize(blocks, carried, rounds):
    squares = jnp.sum(jnp.square(blocks.astype(jnp.float32)), axis=(1, 2))
    total = jnp.sqrt(squares)
    iterate = (blocks.astype(jnp.float32) / (total + NORM_EPSILON)[:, None, None]).astype(
        jnp.bfloat16
    )
    for repeat in range(ITERS):
        carried, iterate = lax.optimization_barrier((carried, iterate))
        for step in rounds[repeat] if repeat < len(rounds) else ():
            carried = step(carried)
        gram = jnp.einsum("kij,klj->kil", iterate, iterate, preferred_element_type=jnp.float32)
        gram_half = gram.astype(jnp.bfloat16)
        square_term = jnp.einsum(
            "kij,kjl->kil", gram_half, gram_half, preferred_element_type=jnp.float32
        )
        poly = (CUBIC_TERM * gram + QUINTIC_TERM * square_term).astype(jnp.bfloat16)
        product = jnp.einsum("kij,kjl->kil", poly, iterate, preferred_element_type=jnp.float32)
        iterate = (LINEAR_TERM * iterate.astype(jnp.float32) + product).astype(jnp.bfloat16)
    for group in rounds[ITERS:]:
        for step in group:
            carried = step(carried)
    return iterate, carried


def butterfly_rounds(axis):
    size = lax.axis_size(axis)
    if size & (size - 1):
        return [lambda value: jnp.sum(lax.all_gather(value, axis, axis=0, tiled=False), axis=0)]
    steps = []
    distance = 1
    while distance < size:
        perm = [(i, i ^ distance) for i in range(size)]
        steps.append(lambda value, perm=perm: value + lax.ppermute(value, axis, perm))
        distance *= 2
    return steps


def vector_partials(normed, ln_gain, ln_bias, ln_cotangent, router_cotangent):
    normed_float = normed.astype(jnp.float32)
    cot_float = ln_cotangent.astype(jnp.float32)
    ln_out = (ln_gain[None, :] * normed_float + ln_bias[None, :]).astype(jnp.bfloat16)
    gain_local = jnp.sum(cot_float * normed_float, axis=0)
    bias_local = jnp.sum(cot_float, axis=0)
    router_local = lax.dot_general(
        router_cotangent, ln_out, (((0,), (0,)), ((), ())), preferred_element_type=jnp.float32
    )
    return jnp.concatenate([gain_local[None, :], bias_local[None, :], router_local], axis=0)


def adam(vec_grad, first_moment, second_moment):
    next_first = ADAM_FIRST * first_moment + (1.0 - ADAM_FIRST) * vec_grad
    next_second = ADAM_SECOND * second_moment + (1.0 - ADAM_SECOND) * vec_grad * vec_grad
    adam_step = next_first / (jnp.sqrt(next_second) + ADAM_EPSILON)
    return next_first, next_second, adam_step


def on_device(
    gradient,
    momentum,
    normed,
    ln_gain,
    ln_bias,
    ln_cotangent,
    router_cotangent,
    first_moment,
    second_moment,
):
    grad_float = gradient.astype(jnp.float32)
    next_momentum = MUON_DECAY * momentum + grad_float
    nesterov = (grad_float + MUON_DECAY * next_momentum).astype(jnp.bfloat16)
    count_all, rows_piece, cols_full = nesterov.shape
    inner = lax.axis_size("inner")
    slots = -(-count_all // inner)
    padded = jnp.pad(nesterov, ((0, slots * inner - count_all), (0, 0), (0, 0)))
    by_owner = padded.reshape(inner, slots, rows_piece, cols_full)
    here = lax.axis_index("inner")
    strip = jnp.concatenate(
        [shift(lax.dynamic_index_in_dim(by_owner, (here + k) % inner, 0, keepdims=False), "inner", k)
         for k in range(inner)],
        axis=1,
    )
    blocks = ring_gather(strip, "outer")
    local = vector_partials(normed, ln_gain, ln_bias, ln_cotangent, router_cotangent)
    steps = [step for axis in ("section",) + SHARD for step in butterfly_rounds(axis)]
    rounds = [steps[:2]] + [[step] for step in steps[2:]]
    result, vec_grad = orthogonalize(blocks, local, rounds)
    next_first, next_second, adam_step = adam(vec_grad, first_moment, second_moment)
    back = jnp.stack(
        [shift(result[:, k * rows_piece:(k + 1) * rows_piece], "inner", -k) for k in range(inner)],
        axis=0,
    )
    twice = jnp.concatenate([back, back], axis=0)
    ordered = lax.dynamic_slice_in_dim(twice, (inner - here) % inner, inner, axis=0)
    ordered = ordered.reshape(inner * slots, rows_piece, cols_full)
    update = ordered[:count_all].astype(jnp.float32) * math.sqrt(FF)
    return (next_momentum, update, next_first, next_second, adam_step)


def inner_size(mesh):
    row = np.asarray(mesh.devices)[:, 0, 0]
    try:
        size = len({tuple(device.coords)[0] for device in row})
    except (AttributeError, TypeError):
        size = 0
    if size <= 1 or row.size % size:
        size = math.gcd(row.size, 4)
    return size


def solution(mesh):
    devices = np.asarray(mesh.devices)
    shard, tensor, section = devices.shape
    inner = inner_size(mesh)
    split = Mesh(
        devices.reshape(shard // inner, inner, tensor, section),
        ("outer", "inner", "tensor", "section"),
    )
    return jax.shard_map(
        on_device,
        mesh=split,
        in_specs=(
            P(("tensor", "section"), SHARD, None),
            P(("tensor", "section"), SHARD, None),
            P((*SHARD, "section"), "tensor"),
            P("tensor"),
            P("tensor"),
            P((*SHARD, "section"), "tensor"),
            P((*SHARD, "section"), None),
            P(None, "tensor"),
            P(None, "tensor"),
        ),
        out_specs=(
            P(("tensor", "section"), SHARD, None),
            P(("tensor", "section"), SHARD, None),
            P(None, "tensor"),
            P(None, "tensor"),
            P(None, "tensor"),
        ),
        check_vma=False,
    )
```

```python
import math

import jax
import jax.numpy as jnp
import numpy as np
from jax import lax
from jax.experimental import pallas as pl
from jax.sharding import Mesh
from jax.sharding import PartitionSpec as P

FF = 2048
ITERS = 5


MUON_DECAY = 0.95
LINEAR_TERM = 3.4445
CUBIC_TERM = -4.775
QUINTIC_TERM = 2.0315
NORM_EPSILON = 1e-07
ADAM_FIRST = 0.9
ADAM_SECOND = 0.95
ADAM_EPSILON = 1e-08

SHARD = ("outer", "inner")


def shift(value, axis, k):
    size = lax.axis_size(axis)
    if k % size == 0:
        return value
    return lax.ppermute(value, axis, [(i, (i + k) % size) for i in range(size)])


def ring_gather(strip, axis):
    size = lax.axis_size(axis)
    cols = strip.shape[-1]
    ahead, behind = [], []
    from_behind = from_ahead = strip
    for distance in range(1, size // 2 + 1):
        if 2 * distance == size:
            half = cols // 2
            first = shift(from_behind[..., :half], axis, 1)
            second = shift(from_ahead[..., half:], axis, -1)
            ahead.append(jnp.concatenate([first, second], axis=-1))
            break
        from_behind = shift(from_behind, axis, 1)
        from_ahead = shift(from_ahead, axis, -1)
        ahead.append(from_ahead)
        behind.append(from_behind)
    return jnp.concatenate([strip] + ahead + behind[::-1], axis=1)


def ns_step_kernel(iterate_ref, out_ref):
    iterate = iterate_ref[...]
    gram = lax.dot_general(
        iterate, iterate, (((1,), (1,)), ((), ())), preferred_element_type=jnp.float32
    )
    gram_half = gram.astype(jnp.bfloat16)
    square_term = jnp.dot(gram_half, gram_half, preferred_element_type=jnp.float32)
    poly = (CUBIC_TERM * gram + QUINTIC_TERM * square_term).astype(jnp.bfloat16)
    product = jnp.dot(poly, iterate, preferred_element_type=jnp.float32)
    out_ref[...] = (LINEAR_TERM * iterate.astype(jnp.float32) + product).astype(jnp.bfloat16)


def ns_step(iterate):
    count, rows, cols = iterate.shape
    spec = pl.BlockSpec((None, rows, cols), lambda k: (k, 0, 0))
    return pl.pallas_call(
        ns_step_kernel,
        out_shape=jax.ShapeDtypeStruct(iterate.shape, iterate.dtype),
        grid=(count,),
        in_specs=[spec],
        out_specs=spec,
    )(iterate)


def orthogonalize(blocks, carried, rounds):
    squares = jnp.sum(jnp.square(blocks.astype(jnp.float32)), axis=(1, 2))
    total = jnp.sqrt(squares)
    iterate = (blocks.astype(jnp.float32) / (total + NORM_EPSILON)[:, None, None]).astype(
        jnp.bfloat16
    )
    for repeat in range(ITERS):
        carried, iterate = lax.optimization_barrier((carried, iterate))
        for step in rounds[repeat] if repeat < len(rounds) else ():
            carried = step(carried)
        iterate = ns_step(iterate)
    for group in rounds[ITERS:]:
        for step in group:
            carried = step(carried)
    return iterate, carried


def butterfly_rounds(axis):
    size = lax.axis_size(axis)
    if size & (size - 1):
        return [lambda value: jnp.sum(lax.all_gather(value, axis, axis=0, tiled=False), axis=0)]
    steps = []
    distance = 1
    while distance < size:
        perm = [(i, i ^ distance) for i in range(size)]
        steps.append(lambda value, perm=perm: value + lax.ppermute(value, axis, perm))
        distance *= 2
    return steps


def vector_partials(normed, ln_gain, ln_bias, ln_cotangent, router_cotangent):
    normed_float = normed.astype(jnp.float32)
    cot_float = ln_cotangent.astype(jnp.float32)
    ln_out = (ln_gain[None, :] * normed_float + ln_bias[None, :]).astype(jnp.bfloat16)
    gain_local = jnp.sum(cot_float * normed_float, axis=0)
    bias_local = jnp.sum(cot_float, axis=0)
    router_local = lax.dot_general(
        router_cotangent, ln_out, (((0,), (0,)), ((), ())), preferred_element_type=jnp.float32
    )
    return jnp.concatenate([gain_local[None, :], bias_local[None, :], router_local], axis=0)


def adam(vec_grad, first_moment, second_moment):
    next_first = ADAM_FIRST * first_moment + (1.0 - ADAM_FIRST) * vec_grad
    next_second = ADAM_SECOND * second_moment + (1.0 - ADAM_SECOND) * vec_grad * vec_grad
    adam_step = next_first / (jnp.sqrt(next_second) + ADAM_EPSILON)
    return next_first, next_second, adam_step


def on_device(
    gradient,
    momentum,
    normed,
    ln_gain,
    ln_bias,
    ln_cotangent,
    router_cotangent,
    first_moment,
    second_moment,
):
    grad_float = gradient.astype(jnp.float32)
    next_momentum = MUON_DECAY * momentum + grad_float
    nesterov = (grad_float + MUON_DECAY * next_momentum).astype(jnp.bfloat16)
    count_all, rows_piece, cols_full = nesterov.shape
    inner = lax.axis_size("inner")
    slots = -(-count_all // inner)
    padded = jnp.pad(nesterov, ((0, slots * inner - count_all), (0, 0), (0, 0)))
    by_owner = padded.reshape(inner, slots, rows_piece, cols_full)
    here = lax.axis_index("inner")
    strip = jnp.concatenate(
        [shift(lax.dynamic_index_in_dim(by_owner, (here + k) % inner, 0, keepdims=False), "inner", k)
         for k in range(inner)],
        axis=1,
    )
    blocks = ring_gather(strip, "outer")
    local = vector_partials(normed, ln_gain, ln_bias, ln_cotangent, router_cotangent)
    steps = [step for axis in ("section",) + SHARD for step in butterfly_rounds(axis)]
    rounds = [steps[:2]] + [[step] for step in steps[2:]]
    result, vec_grad = orthogonalize(blocks, local, rounds)
    next_first, next_second, adam_step = adam(vec_grad, first_moment, second_moment)
    back = jnp.stack(
        [shift(result[:, k * rows_piece:(k + 1) * rows_piece], "inner", -k) for k in range(inner)],
        axis=0,
    )
    twice = jnp.concatenate([back, back], axis=0)
    ordered = lax.dynamic_slice_in_dim(twice, (inner - here) % inner, inner, axis=0)
    ordered = ordered.reshape(inner * slots, rows_piece, cols_full)
    update = ordered[:count_all].astype(jnp.float32) * math.sqrt(FF)
    return (next_momentum, update, next_first, next_second, adam_step)


def inner_size(mesh):
    row = np.asarray(mesh.devices)[:, 0, 0]
    try:
        size = len({tuple(device.coords)[0] for device in row})
    except (AttributeError, TypeError):
        size = 0
    if size <= 1 or row.size % size:
        size = math.gcd(row.size, 4)
    return size


def solution(mesh):
    devices = np.asarray(mesh.devices)
    shard, tensor, section = devices.shape
    inner = inner_size(mesh)
    split = Mesh(
        devices.reshape(shard // inner, inner, tensor, section),
        ("outer", "inner", "tensor", "section"),
    )
    return jax.shard_map(
        on_device,
        mesh=split,
        in_specs=(
            P(("tensor", "section"), SHARD, None),
            P(("tensor", "section"), SHARD, None),
            P((*SHARD, "section"), "tensor"),
            P("tensor"),
            P("tensor"),
            P((*SHARD, "section"), "tensor"),
            P((*SHARD, "section"), None),
            P(None, "tensor"),
            P(None, "tensor"),
        ),
        out_specs=(
            P(("tensor", "section"), SHARD, None),
            P(("tensor", "section"), SHARD, None),
            P(None, "tensor"),
            P(None, "tensor"),
            P(None, "tensor"),
        ),
        check_vma=False,
    )
```

```python
import math

import jax
import jax.numpy as jnp
import numpy as np
from jax import lax
from jax.sharding import Mesh
from jax.sharding import PartitionSpec as P

FF = 2048
ITERS = 5


MUON_DECAY = 0.95
LINEAR_TERM = 3.4445
CUBIC_TERM = -4.775
QUINTIC_TERM = 2.0315
NORM_EPSILON = 1e-07
ADAM_FIRST = 0.9
ADAM_SECOND = 0.95
ADAM_EPSILON = 1e-08

SHARD = ("outer", "inner")


def shift(value, axis, k):
    size = lax.axis_size(axis)
    if k % size == 0:
        return value
    return lax.ppermute(value, axis, [(i, (i + k) % size) for i in range(size)])


def ring_gather(strip, extra, axis):
    size = lax.axis_size(axis)
    cols = strip.shape[-1]
    ahead, behind = [], []
    from_behind = from_ahead = (strip, extra)
    for distance in range(1, size // 2 + 1):
        if 2 * distance == size:
            half = cols // 2
            first, far_extra = shift((from_behind[0][..., :half], from_behind[1]), axis, 1)
            second = shift(from_ahead[0][..., half:], axis, -1)
            ahead.append((jnp.concatenate([first, second], axis=-1), far_extra))
            break
        from_behind = shift(from_behind, axis, 1)
        from_ahead = shift(from_ahead, axis, -1)
        ahead.append(from_ahead)
        behind.append(from_behind)
    pieces = [(strip, extra)] + ahead + behind[::-1]
    return jnp.concatenate([p[0] for p in pieces], axis=1), [p[1] for p in pieces]


def ordered_sum(by_offset, axis):
    size = lax.axis_size(axis)
    stacked = jnp.stack(by_offset, axis=0)
    place = (jnp.arange(size) - lax.axis_index(axis)) % size
    in_order = jnp.take(stacked, place, axis=0)
    total = in_order[0]
    for index in range(1, size):
        total = total + in_order[index]
    return total


def orthogonalize(blocks, carried, rounds):
    squares = jnp.sum(jnp.square(blocks.astype(jnp.float32)), axis=(1, 2))
    total = jnp.sqrt(squares)
    iterate = (blocks.astype(jnp.float32) / (total + NORM_EPSILON)[:, None, None]).astype(
        jnp.bfloat16
    )
    for repeat in range(ITERS):
        carried, iterate = lax.optimization_barrier((carried, iterate))
        for step in rounds[repeat] if repeat < len(rounds) else ():
            carried = step(carried)
        gram = jnp.einsum("kij,klj->kil", iterate, iterate, preferred_element_type=jnp.float32)
        gram_half = gram.astype(jnp.bfloat16)
        square_term = jnp.einsum(
            "kij,kjl->kil", gram_half, gram_half, preferred_element_type=jnp.float32
        )
        poly = (CUBIC_TERM * gram + QUINTIC_TERM * square_term).astype(jnp.bfloat16)
        product = jnp.einsum("kij,kjl->kil", poly, iterate, preferred_element_type=jnp.float32)
        iterate = (LINEAR_TERM * iterate.astype(jnp.float32) + product).astype(jnp.bfloat16)
    for group in rounds[ITERS:]:
        for step in group:
            carried = step(carried)
    return iterate, carried


def butterfly_rounds(axis):
    size = lax.axis_size(axis)
    if size & (size - 1):
        return [lambda value: jnp.sum(lax.all_gather(value, axis, axis=0, tiled=False), axis=0)]
    steps = []
    distance = 1
    while distance < size:
        perm = [(i, i ^ distance) for i in range(size)]
        steps.append(lambda value, perm=perm: value + lax.ppermute(value, axis, perm))
        distance *= 2
    return steps


def vector_partials(normed, ln_gain, ln_bias, ln_cotangent, router_cotangent):
    normed_float = normed.astype(jnp.float32)
    cot_float = ln_cotangent.astype(jnp.float32)
    ln_out = (ln_gain[None, :] * normed_float + ln_bias[None, :]).astype(jnp.bfloat16)
    gain_local = jnp.sum(cot_float * normed_float, axis=0)
    bias_local = jnp.sum(cot_float, axis=0)
    router_local = lax.dot_general(
        router_cotangent, ln_out, (((0,), (0,)), ((), ())), preferred_element_type=jnp.float32
    )
    return jnp.concatenate([gain_local[None, :], bias_local[None, :], router_local], axis=0)


def adam(vec_grad, first_moment, second_moment):
    next_first = ADAM_FIRST * first_moment + (1.0 - ADAM_FIRST) * vec_grad
    next_second = ADAM_SECOND * second_moment + (1.0 - ADAM_SECOND) * vec_grad * vec_grad
    adam_step = next_first / (jnp.sqrt(next_second) + ADAM_EPSILON)
    return next_first, next_second, adam_step


def on_device(
    gradient,
    momentum,
    normed,
    ln_gain,
    ln_bias,
    ln_cotangent,
    router_cotangent,
    first_moment,
    second_moment,
):
    grad_float = gradient.astype(jnp.float32)
    next_momentum = MUON_DECAY * momentum + grad_float
    nesterov = (grad_float + MUON_DECAY * next_momentum).astype(jnp.bfloat16)
    count_all, rows_piece, cols_full = nesterov.shape
    inner = lax.axis_size("inner")
    slots = -(-count_all // inner)
    padded = jnp.pad(nesterov, ((0, slots * inner - count_all), (0, 0), (0, 0)))
    by_owner = padded.reshape(inner, slots, rows_piece, cols_full)
    here = lax.axis_index("inner")
    local = vector_partials(normed, ln_gain, ln_bias, ln_cotangent, router_cotangent)
    moved = [
        shift((lax.dynamic_index_in_dim(by_owner, (here + k) % inner, 0, keepdims=False), local),
              "inner", k)
        for k in range(inner)
    ]
    strip = jnp.concatenate([piece for piece, _ in moved], axis=1)
    inner_sum = ordered_sum([moved[(-k) % inner][1] for k in range(inner)], "inner")
    blocks, outer_sums = ring_gather(strip, inner_sum, "outer")
    outer_sum = ordered_sum(outer_sums, "outer")
    rounds = [butterfly_rounds("section")]
    result, vec_grad = orthogonalize(blocks, outer_sum, rounds)
    next_first, next_second, adam_step = adam(vec_grad, first_moment, second_moment)
    back = jnp.stack(
        [shift(result[:, k * rows_piece:(k + 1) * rows_piece], "inner", -k) for k in range(inner)],
        axis=0,
    )
    twice = jnp.concatenate([back, back], axis=0)
    ordered = lax.dynamic_slice_in_dim(twice, (inner - here) % inner, inner, axis=0)
    ordered = ordered.reshape(inner * slots, rows_piece, cols_full)
    update = ordered[:count_all].astype(jnp.float32) * math.sqrt(FF)
    return (next_momentum, update, next_first, next_second, adam_step)


def inner_size(mesh):
    row = np.asarray(mesh.devices)[:, 0, 0]
    try:
        size = len({tuple(device.coords)[0] for device in row})
    except (AttributeError, TypeError):
        size = 0
    if size <= 1 or row.size % size:
        size = math.gcd(row.size, 4)
    return size


def solution(mesh):
    devices = np.asarray(mesh.devices)
    shard, tensor, section = devices.shape
    inner = inner_size(mesh)
    split = Mesh(
        devices.reshape(shard // inner, inner, tensor, section),
        ("outer", "inner", "tensor", "section"),
    )
    return jax.shard_map(
        on_device,
        mesh=split,
        in_specs=(
            P(("tensor", "section"), SHARD, None),
            P(("tensor", "section"), SHARD, None),
            P((*SHARD, "section"), "tensor"),
            P("tensor"),
            P("tensor"),
            P((*SHARD, "section"), "tensor"),
            P((*SHARD, "section"), None),
            P(None, "tensor"),
            P(None, "tensor"),
        ),
        out_specs=(
            P(("tensor", "section"), SHARD, None),
            P(("tensor", "section"), SHARD, None),
            P(None, "tensor"),
            P(None, "tensor"),
            P(None, "tensor"),
        ),
        check_vma=False,
    )
```

```python
import math

import jax
import jax.numpy as jnp
import numpy as np
from jax import lax
from jax.experimental import pallas as pl
from jax.experimental.pallas import tpu as pltpu
from jax.sharding import Mesh
from jax.sharding import PartitionSpec as P

FF = 2048
ITERS = 5


MUON_DECAY = 0.95
LINEAR_TERM = 3.4445
CUBIC_TERM = -4.775
QUINTIC_TERM = 2.0315
NORM_EPSILON = 1e-07
ADAM_FIRST = 0.9
ADAM_SECOND = 0.95
ADAM_EPSILON = 1e-08

SHARD = ("outer", "inner")


def shift(value, axis, k):
    size = lax.axis_size(axis)
    if k % size == 0:
        return value
    return lax.ppermute(value, axis, [(i, (i + k) % size) for i in range(size)])


def ring_gather(strip, axis):
    size = lax.axis_size(axis)
    cols = strip.shape[-1]
    ahead, behind = [], []
    from_behind = from_ahead = strip
    for distance in range(1, size // 2 + 1):
        if 2 * distance == size:
            half = cols // 2
            first = shift(from_behind[..., :half], axis, 1)
            second = shift(from_ahead[..., half:], axis, -1)
            ahead.append(jnp.concatenate([first, second], axis=-1))
            break
        from_behind = shift(from_behind, axis, 1)
        from_ahead = shift(from_ahead, axis, -1)
        ahead.append(from_ahead)
        behind.append(from_behind)
    return jnp.concatenate([strip] + ahead + behind[::-1], axis=1)


def ns_update(iterate):
    gram = lax.dot_general(
        iterate, iterate, (((1,), (1,)), ((), ())), preferred_element_type=jnp.float32
    )
    gram_half = gram.astype(jnp.bfloat16)
    square_term = jnp.dot(gram_half, gram_half, preferred_element_type=jnp.float32)
    poly = (CUBIC_TERM * gram + QUINTIC_TERM * square_term).astype(jnp.bfloat16)
    product = jnp.dot(poly, iterate, preferred_element_type=jnp.float32)
    return (LINEAR_TERM * iterate.astype(jnp.float32) + product).astype(jnp.bfloat16)


def first_step_kernel(blocks_ref, out_ref):
    for k in range(blocks_ref.shape[0]):
        wide = blocks_ref[k].astype(jnp.float32)
        total = jnp.sqrt(jnp.sum(wide * wide))
        out_ref[k] = ns_update((wide / (total + NORM_EPSILON)).astype(jnp.bfloat16))


def later_step_kernel(iterate_ref, out_ref):
    for k in range(iterate_ref.shape[0]):
        out_ref[k] = ns_update(iterate_ref[k])


def in_vmem(resident):
    return pl.BlockSpec(memory_space=pltpu.VMEM) if resident else pl.BlockSpec()


def ns_call(kernel, value, source, target):
    return pl.pallas_call(
        kernel,
        out_shape=jax.ShapeDtypeStruct(value.shape, jnp.bfloat16),
        in_specs=[in_vmem(source)],
        out_specs=in_vmem(target),
    )(value)


def orthogonalize(blocks, carried, rounds):
    iterate = blocks
    for repeat in range(ITERS):
        carried, iterate = lax.optimization_barrier((carried, iterate))
        for step in rounds[repeat] if repeat < len(rounds) else ():
            carried = step(carried)
        kernel = first_step_kernel if repeat == 0 else later_step_kernel
        source = repeat > 0
        target = repeat < ITERS - 1
        iterate = ns_call(kernel, iterate, source, target)
    for group in rounds[ITERS:]:
        for step in group:
            carried = step(carried)
    return iterate, carried


def butterfly_rounds(axis):
    size = lax.axis_size(axis)
    if size & (size - 1):
        return [lambda value: jnp.sum(lax.all_gather(value, axis, axis=0, tiled=False), axis=0)]
    steps = []
    distance = 1
    while distance < size:
        perm = [(i, i ^ distance) for i in range(size)]
        steps.append(lambda value, perm=perm: value + lax.ppermute(value, axis, perm))
        distance *= 2
    return steps


def vector_partials(normed, ln_gain, ln_bias, ln_cotangent, router_cotangent):
    normed_float = normed.astype(jnp.float32)
    cot_float = ln_cotangent.astype(jnp.float32)
    ln_out = (ln_gain[None, :] * normed_float + ln_bias[None, :]).astype(jnp.bfloat16)
    gain_local = jnp.sum(cot_float * normed_float, axis=0)
    bias_local = jnp.sum(cot_float, axis=0)
    router_local = lax.dot_general(
        router_cotangent, ln_out, (((0,), (0,)), ((), ())), preferred_element_type=jnp.float32
    )
    return jnp.concatenate([gain_local[None, :], bias_local[None, :], router_local], axis=0)


def adam(vec_grad, first_moment, second_moment):
    next_first = ADAM_FIRST * first_moment + (1.0 - ADAM_FIRST) * vec_grad
    next_second = ADAM_SECOND * second_moment + (1.0 - ADAM_SECOND) * vec_grad * vec_grad
    adam_step = next_first / (jnp.sqrt(next_second) + ADAM_EPSILON)
    return next_first, next_second, adam_step


def on_device(
    gradient,
    momentum,
    normed,
    ln_gain,
    ln_bias,
    ln_cotangent,
    router_cotangent,
    first_moment,
    second_moment,
):
    grad_float = gradient.astype(jnp.float32)
    next_momentum = MUON_DECAY * momentum + grad_float
    nesterov = (grad_float + MUON_DECAY * next_momentum).astype(jnp.bfloat16)
    count_all, rows_piece, cols_full = nesterov.shape
    inner = lax.axis_size("inner")
    slots = -(-count_all // inner)
    padded = jnp.pad(nesterov, ((0, slots * inner - count_all), (0, 0), (0, 0)))
    by_owner = padded.reshape(inner, slots, rows_piece, cols_full)
    here = lax.axis_index("inner")
    strip = jnp.concatenate(
        [shift(lax.dynamic_index_in_dim(by_owner, (here + k) % inner, 0, keepdims=False), "inner", k)
         for k in range(inner)],
        axis=1,
    )
    blocks = ring_gather(strip, "outer")
    local = vector_partials(normed, ln_gain, ln_bias, ln_cotangent, router_cotangent)
    steps = [step for axis in ("section",) + SHARD for step in butterfly_rounds(axis)]
    rounds = [steps[:2]] + [[step] for step in steps[2:]]
    result, vec_grad = orthogonalize(blocks, local, rounds)
    next_first, next_second, adam_step = adam(vec_grad, first_moment, second_moment)
    back = jnp.stack(
        [shift(result[:, k * rows_piece:(k + 1) * rows_piece], "inner", -k) for k in range(inner)],
        axis=0,
    )
    twice = jnp.concatenate([back, back], axis=0)
    ordered = lax.dynamic_slice_in_dim(twice, (inner - here) % inner, inner, axis=0)
    ordered = ordered.reshape(inner * slots, rows_piece, cols_full)
    update = ordered[:count_all].astype(jnp.float32) * math.sqrt(FF)
    return (next_momentum, update, next_first, next_second, adam_step)


def inner_size(mesh):
    row = np.asarray(mesh.devices)[:, 0, 0]
    try:
        size = len({tuple(device.coords)[0] for device in row})
    except (AttributeError, TypeError):
        size = 0
    if size <= 1 or row.size % size:
        size = math.gcd(row.size, 4)
    return size


def solution(mesh):
    devices = np.asarray(mesh.devices)
    shard, tensor, section = devices.shape
    inner = inner_size(mesh)
    split = Mesh(
        devices.reshape(shard // inner, inner, tensor, section),
        ("outer", "inner", "tensor", "section"),
    )
    return jax.shard_map(
        on_device,
        mesh=split,
        in_specs=(
            P(("tensor", "section"), SHARD, None),
            P(("tensor", "section"), SHARD, None),
            P((*SHARD, "section"), "tensor"),
            P("tensor"),
            P("tensor"),
            P((*SHARD, "section"), "tensor"),
            P((*SHARD, "section"), None),
            P(None, "tensor"),
            P(None, "tensor"),
        ),
        out_specs=(
            P(("tensor", "section"), SHARD, None),
            P(("tensor", "section"), SHARD, None),
            P(None, "tensor"),
            P(None, "tensor"),
            P(None, "tensor"),
        ),
        check_vma=False,
    )
```

```python
import math

import jax
import jax.numpy as jnp
import numpy as np
from jax import lax
from jax.sharding import Mesh
from jax.sharding import PartitionSpec as P

FF = 2048
ITERS = 5


MUON_DECAY = 0.95
LINEAR_TERM = 3.4445
CUBIC_TERM = -4.775
QUINTIC_TERM = 2.0315
NORM_EPSILON = 1e-07
ADAM_FIRST = 0.9
ADAM_SECOND = 0.95
ADAM_EPSILON = 1e-08

SHARD = ("outer", "inner")


def shift(value, axis, k):
    size = lax.axis_size(axis)
    if k % size == 0:
        return value
    return lax.ppermute(value, axis, [(i, (i + k) % size) for i in range(size)])


def ring_gather(strip, axis):
    size = lax.axis_size(axis)
    cols = strip.shape[-1]
    ahead, behind = [], []
    from_behind = from_ahead = strip
    for distance in range(1, size // 2 + 1):
        if 2 * distance == size:
            half = cols // 2
            first = shift(from_behind[..., :half], axis, 1)
            second = shift(from_ahead[..., half:], axis, -1)
            ahead.append(jnp.concatenate([first, second], axis=-1))
            break
        from_behind = shift(from_behind, axis, 1)
        from_ahead = shift(from_ahead, axis, -1)
        ahead.append(from_ahead)
        behind.append(from_behind)
    return jnp.concatenate([strip] + ahead + behind[::-1], axis=1)


def orthogonalize(blocks, carried, rounds, keep):
    squares = jnp.sum(jnp.square(blocks.astype(jnp.float32)), axis=(1, 2))
    total = jnp.sqrt(squares)
    iterate = (blocks.astype(jnp.float32) / (total + NORM_EPSILON)[:, None, None]).astype(
        jnp.bfloat16
    )
    for repeat in range(ITERS):
        carried, iterate = lax.optimization_barrier((carried, iterate))
        for step in rounds[repeat] if repeat < len(rounds) else ():
            carried = step(carried)
        gram = jnp.einsum("kij,klj->kil", iterate, iterate, preferred_element_type=jnp.float32)
        gram_half = gram.astype(jnp.bfloat16)
        rows = keep if repeat == ITERS - 1 else iterate.shape[1]
        square_term = jnp.einsum(
            "kij,kjl->kil", gram_half[:, :rows], gram_half, preferred_element_type=jnp.float32
        )
        poly = (CUBIC_TERM * gram[:, :rows] + QUINTIC_TERM * square_term).astype(jnp.bfloat16)
        product = jnp.einsum("kij,kjl->kil", poly, iterate, preferred_element_type=jnp.float32)
        iterate = (LINEAR_TERM * iterate[:, :rows].astype(jnp.float32) + product).astype(
            jnp.bfloat16
        )
    for group in rounds[ITERS:]:
        for step in group:
            carried = step(carried)
    return iterate, carried


def butterfly_rounds(axis):
    size = lax.axis_size(axis)
    if size & (size - 1):
        return [lambda value: jnp.sum(lax.all_gather(value, axis, axis=0, tiled=False), axis=0)]
    steps = []
    distance = 1
    while distance < size:
        perm = [(i, i ^ distance) for i in range(size)]
        steps.append(lambda value, perm=perm: value + lax.ppermute(value, axis, perm))
        distance *= 2
    return steps


def vector_partials(normed, ln_gain, ln_bias, ln_cotangent, router_cotangent):
    normed_float = normed.astype(jnp.float32)
    cot_float = ln_cotangent.astype(jnp.float32)
    ln_out = (ln_gain[None, :] * normed_float + ln_bias[None, :]).astype(jnp.bfloat16)
    gain_local = jnp.sum(cot_float * normed_float, axis=0)
    bias_local = jnp.sum(cot_float, axis=0)
    router_local = lax.dot_general(
        router_cotangent, ln_out, (((0,), (0,)), ((), ())), preferred_element_type=jnp.float32
    )
    return jnp.concatenate([gain_local[None, :], bias_local[None, :], router_local], axis=0)


def adam(vec_grad, first_moment, second_moment):
    next_first = ADAM_FIRST * first_moment + (1.0 - ADAM_FIRST) * vec_grad
    next_second = ADAM_SECOND * second_moment + (1.0 - ADAM_SECOND) * vec_grad * vec_grad
    adam_step = next_first / (jnp.sqrt(next_second) + ADAM_EPSILON)
    return next_first, next_second, adam_step


def on_device(
    gradient,
    momentum,
    normed,
    ln_gain,
    ln_bias,
    ln_cotangent,
    router_cotangent,
    first_moment,
    second_moment,
):
    grad_float = gradient.astype(jnp.float32)
    next_momentum = MUON_DECAY * momentum + grad_float
    nesterov = (grad_float + MUON_DECAY * next_momentum).astype(jnp.bfloat16)
    count_all, rows_piece, cols_full = nesterov.shape
    inner = lax.axis_size("inner")
    slots = -(-count_all // inner)
    padded = jnp.pad(nesterov, ((0, slots * inner - count_all), (0, 0), (0, 0)))
    by_owner = padded.reshape(inner, slots, rows_piece, cols_full)
    here = lax.axis_index("inner")
    strip = jnp.concatenate(
        [shift(lax.dynamic_index_in_dim(by_owner, (here + k) % inner, 0, keepdims=False), "inner", k)
         for k in range(inner)],
        axis=1,
    )
    blocks = ring_gather(strip, "outer")
    local = vector_partials(normed, ln_gain, ln_bias, ln_cotangent, router_cotangent)
    steps = [step for axis in ("section",) + SHARD for step in butterfly_rounds(axis)]
    rounds = [steps[:2]] + [[step] for step in steps[2:]]
    result, vec_grad = orthogonalize(blocks, local, rounds, inner * rows_piece)
    next_first, next_second, adam_step = adam(vec_grad, first_moment, second_moment)
    back = jnp.stack(
        [shift(result[:, k * rows_piece:(k + 1) * rows_piece], "inner", -k) for k in range(inner)],
        axis=0,
    )
    twice = jnp.concatenate([back, back], axis=0)
    ordered = lax.dynamic_slice_in_dim(twice, (inner - here) % inner, inner, axis=0)
    ordered = ordered.reshape(inner * slots, rows_piece, cols_full)
    update = ordered[:count_all].astype(jnp.float32) * math.sqrt(FF)
    return (next_momentum, update, next_first, next_second, adam_step)


def inner_size(mesh):
    row = np.asarray(mesh.devices)[:, 0, 0]
    try:
        size = len({tuple(device.coords)[0] for device in row})
    except (AttributeError, TypeError):
        size = 0
    if size <= 1 or row.size % size:
        size = math.gcd(row.size, 4)
    return size


def solution(mesh):
    devices = np.asarray(mesh.devices)
    shard, tensor, section = devices.shape
    inner = inner_size(mesh)
    split = Mesh(
        devices.reshape(shard // inner, inner, tensor, section),
        ("outer", "inner", "tensor", "section"),
    )
    return jax.shard_map(
        on_device,
        mesh=split,
        in_specs=(
            P(("tensor", "section"), SHARD, None),
            P(("tensor", "section"), SHARD, None),
            P((*SHARD, "section"), "tensor"),
            P("tensor"),
            P("tensor"),
            P((*SHARD, "section"), "tensor"),
            P((*SHARD, "section"), None),
            P(None, "tensor"),
            P(None, "tensor"),
        ),
        out_specs=(
            P(("tensor", "section"), SHARD, None),
            P(("tensor", "section"), SHARD, None),
            P(None, "tensor"),
            P(None, "tensor"),
            P(None, "tensor"),
        ),
        check_vma=False,
    )
```

```python
import math

import jax
import jax.numpy as jnp
import numpy as np
from jax import lax
from jax.sharding import Mesh
from jax.sharding import PartitionSpec as P

FF = 2048
ITERS = 5


MUON_DECAY = 0.95
LINEAR_TERM = 3.4445
CUBIC_TERM = -4.775
QUINTIC_TERM = 2.0315
NORM_EPSILON = 1e-07
ADAM_FIRST = 0.9
ADAM_SECOND = 0.95
ADAM_EPSILON = 1e-08

SHARD = ("outer", "inner")


def shift(value, axis, k):
    size = lax.axis_size(axis)
    if k % size == 0:
        return value
    return lax.ppermute(value, axis, [(i, (i + k) % size) for i in range(size)])


def ring_gather(strip, axis):
    size = lax.axis_size(axis)
    cols = strip.shape[-1]
    ahead, behind = [], []
    from_behind = from_ahead = strip
    for distance in range(1, size // 2 + 1):
        if 2 * distance == size:
            half = cols // 2
            first = shift(from_behind[..., :half], axis, 1)
            second = shift(from_ahead[..., half:], axis, -1)
            ahead.append(jnp.concatenate([first, second], axis=-1))
            break
        from_behind = shift(from_behind, axis, 1)
        from_ahead = shift(from_ahead, axis, -1)
        ahead.append(from_ahead)
        behind.append(from_behind)
    return jnp.concatenate([strip] + ahead + behind[::-1], axis=1)


EXTRA_ROWS = 8


def encode(value, like):
    flat = value.reshape(-1)
    high = flat.astype(jnp.bfloat16)
    low = (flat - high.astype(jnp.float32)).astype(jnp.bfloat16)
    slots, _, cols = like.shape
    room = EXTRA_ROWS * cols - 2 * flat.size
    packed = jnp.concatenate([high, low, jnp.zeros((room,), jnp.bfloat16)])
    return jnp.broadcast_to(packed.reshape(1, EXTRA_ROWS, cols), (slots, EXTRA_ROWS, cols))


def decode(rows, shape):
    flat = rows[0].reshape(-1)
    size = math.prod(shape)
    high = flat[:size].astype(jnp.float32)
    low = flat[size:2 * size].astype(jnp.float32)
    return (high + low).reshape(shape)


def ordered_sum(by_offset, axis):
    size = lax.axis_size(axis)
    stacked = jnp.stack(by_offset, axis=0)
    place = (jnp.arange(size) - lax.axis_index(axis)) % size
    in_order = jnp.take(stacked, place, axis=0)
    total = in_order[0]
    for index in range(1, size):
        total = total + in_order[index]
    return total


def orthogonalize(blocks, carried, rounds, keep):
    squares = jnp.sum(jnp.square(blocks.astype(jnp.float32)), axis=(1, 2))
    total = jnp.sqrt(squares)
    iterate = (blocks.astype(jnp.float32) / (total + NORM_EPSILON)[:, None, None]).astype(
        jnp.bfloat16
    )
    for repeat in range(ITERS):
        carried, iterate = lax.optimization_barrier((carried, iterate))
        for step in rounds[repeat] if repeat < len(rounds) else ():
            carried = step(carried)
        gram = jnp.einsum("kij,klj->kil", iterate, iterate, preferred_element_type=jnp.float32)
        gram_half = gram.astype(jnp.bfloat16)
        rows = keep if repeat == ITERS - 1 else iterate.shape[1]
        square_term = jnp.einsum(
            "kij,kjl->kil", gram_half[:, :rows], gram_half, preferred_element_type=jnp.float32
        )
        poly = (CUBIC_TERM * gram[:, :rows] + QUINTIC_TERM * square_term).astype(jnp.bfloat16)
        product = jnp.einsum("kij,kjl->kil", poly, iterate, preferred_element_type=jnp.float32)
        iterate = (LINEAR_TERM * iterate[:, :rows].astype(jnp.float32) + product).astype(
            jnp.bfloat16
        )
    for group in rounds[ITERS:]:
        for step in group:
            carried = step(carried)
    return iterate, carried


def butterfly_rounds(axis):
    size = lax.axis_size(axis)
    if size & (size - 1):
        return [lambda value: jnp.sum(lax.all_gather(value, axis, axis=0, tiled=False), axis=0)]
    steps = []
    distance = 1
    while distance < size:
        perm = [(i, i ^ distance) for i in range(size)]
        steps.append(lambda value, perm=perm: value + lax.ppermute(value, axis, perm))
        distance *= 2
    return steps


def vector_partials(normed, ln_gain, ln_bias, ln_cotangent, router_cotangent):
    normed_float = normed.astype(jnp.float32)
    cot_float = ln_cotangent.astype(jnp.float32)
    ln_out = (ln_gain[None, :] * normed_float + ln_bias[None, :]).astype(jnp.bfloat16)
    gain_local = jnp.sum(cot_float * normed_float, axis=0)
    bias_local = jnp.sum(cot_float, axis=0)
    router_local = lax.dot_general(
        router_cotangent, ln_out, (((0,), (0,)), ((), ())), preferred_element_type=jnp.float32
    )
    return jnp.concatenate([gain_local[None, :], bias_local[None, :], router_local], axis=0)


def adam(vec_grad, first_moment, second_moment):
    next_first = ADAM_FIRST * first_moment + (1.0 - ADAM_FIRST) * vec_grad
    next_second = ADAM_SECOND * second_moment + (1.0 - ADAM_SECOND) * vec_grad * vec_grad
    adam_step = next_first / (jnp.sqrt(next_second) + ADAM_EPSILON)
    return next_first, next_second, adam_step


def on_device(
    gradient,
    momentum,
    normed,
    ln_gain,
    ln_bias,
    ln_cotangent,
    router_cotangent,
    first_moment,
    second_moment,
):
    grad_float = gradient.astype(jnp.float32)
    next_momentum = MUON_DECAY * momentum + grad_float
    nesterov = (grad_float + MUON_DECAY * next_momentum).astype(jnp.bfloat16)
    count_all, rows_piece, cols_full = nesterov.shape
    inner = lax.axis_size("inner")
    slots = -(-count_all // inner)
    padded = jnp.pad(nesterov, ((0, slots * inner - count_all), (0, 0), (0, 0)))
    by_owner = padded.reshape(inner, slots, rows_piece, cols_full)
    here = lax.axis_index("inner")
    local = vector_partials(normed, ln_gain, ln_bias, ln_cotangent, router_cotangent)
    shape = local.shape
    extra = encode(local, by_owner[0])
    moved = [
        shift(jnp.concatenate(
            [lax.dynamic_index_in_dim(by_owner, (here + k) % inner, 0, keepdims=False), extra],
            axis=1), "inner", k)
        for k in range(inner)
    ]
    strip = jnp.concatenate([piece[:, :rows_piece] for piece in moved], axis=1)
    inner_sum = ordered_sum(
        [decode(moved[(-k) % inner][:, rows_piece:], shape) for k in range(inner)], "inner"
    )
    strip_rows = inner * rows_piece
    gathered = ring_gather(jnp.concatenate([strip, encode(inner_sum, strip)], axis=1), "outer")
    size = lax.axis_size("outer")
    whole = strip_rows + EXTRA_ROWS
    pieces = [gathered[:, k * whole:(k + 1) * whole] for k in range(size)]
    blocks = jnp.concatenate([piece[:, :strip_rows] for piece in pieces], axis=1)
    outer_sum = ordered_sum([decode(piece[:, strip_rows:], shape) for piece in pieces], "outer")
    rounds = [butterfly_rounds("section")]
    result, vec_grad = orthogonalize(blocks, outer_sum, rounds, strip_rows)
    next_first, next_second, adam_step = adam(vec_grad, first_moment, second_moment)
    back = jnp.stack(
        [shift(result[:, k * rows_piece:(k + 1) * rows_piece], "inner", -k) for k in range(inner)],
        axis=0,
    )
    twice = jnp.concatenate([back, back], axis=0)
    ordered = lax.dynamic_slice_in_dim(twice, (inner - here) % inner, inner, axis=0)
    ordered = ordered.reshape(inner * slots, rows_piece, cols_full)
    update = ordered[:count_all].astype(jnp.float32) * math.sqrt(FF)
    return (next_momentum, update, next_first, next_second, adam_step)


def inner_size(mesh):
    row = np.asarray(mesh.devices)[:, 0, 0]
    try:
        size = len({tuple(device.coords)[0] for device in row})
    except (AttributeError, TypeError):
        size = 0
    if size <= 1 or row.size % size:
        size = math.gcd(row.size, 4)
    return size


def solution(mesh):
    devices = np.asarray(mesh.devices)
    shard, tensor, section = devices.shape
    inner = inner_size(mesh)
    split = Mesh(
        devices.reshape(shard // inner, inner, tensor, section),
        ("outer", "inner", "tensor", "section"),
    )
    return jax.shard_map(
        on_device,
        mesh=split,
        in_specs=(
            P(("tensor", "section"), SHARD, None),
            P(("tensor", "section"), SHARD, None),
            P((*SHARD, "section"), "tensor"),
            P("tensor"),
            P("tensor"),
            P((*SHARD, "section"), "tensor"),
            P((*SHARD, "section"), None),
            P(None, "tensor"),
            P(None, "tensor"),
        ),
        out_specs=(
            P(("tensor", "section"), SHARD, None),
            P(("tensor", "section"), SHARD, None),
            P(None, "tensor"),
            P(None, "tensor"),
            P(None, "tensor"),
        ),
        check_vma=False,
    )
```

```python
import math

import jax
import jax.numpy as jnp
import numpy as np
from jax import lax
from jax.sharding import Mesh
from jax.sharding import PartitionSpec as P

FF = 2048
ITERS = 5


MUON_DECAY = 0.95
LINEAR_TERM = 3.4445
CUBIC_TERM = -4.775
QUINTIC_TERM = 2.0315
NORM_EPSILON = 1e-07
ADAM_FIRST = 0.9
ADAM_SECOND = 0.95
ADAM_EPSILON = 1e-08

SHARD = ("outer", "inner")


def shift(value, axis, k):
    size = lax.axis_size(axis)
    if k % size == 0:
        return value
    return lax.ppermute(value, axis, [(i, (i + k) % size) for i in range(size)])


def ring_gather(strip, axis):
    size = lax.axis_size(axis)
    cols = strip.shape[-1]
    ahead, behind = [], []
    from_behind = from_ahead = strip
    for distance in range(1, size // 2 + 1):
        if 2 * distance == size:
            half = cols // 2
            first = shift(from_behind[..., :half], axis, 1)
            second = shift(from_ahead[..., half:], axis, -1)
            ahead.append(jnp.concatenate([first, second], axis=-1))
            break
        from_behind = shift(from_behind, axis, 1)
        from_ahead = shift(from_ahead, axis, -1)
        ahead.append(from_ahead)
        behind.append(from_behind)
    return jnp.concatenate([strip] + ahead + behind[::-1], axis=1)


def orthogonalize(blocks, carried, rounds, keep):
    squares = jnp.sum(jnp.square(blocks.astype(jnp.float32)), axis=(1, 2))
    total = jnp.sqrt(squares)
    iterate = (blocks.astype(jnp.float32) / (total + NORM_EPSILON)[:, None, None]).astype(
        jnp.bfloat16
    )
    for repeat in range(ITERS):
        carried, iterate = lax.optimization_barrier((carried, iterate))
        for step in rounds[repeat] if repeat < len(rounds) else ():
            carried = step(carried)
        gram = jnp.einsum("kij,klj->kil", iterate, iterate, preferred_element_type=jnp.float32)
        gram_half = gram.astype(jnp.bfloat16)
        rows = keep if repeat == ITERS - 1 else iterate.shape[1]
        square_term = jnp.einsum(
            "kij,kjl->kil", gram_half[:, :rows], gram_half, preferred_element_type=jnp.float32
        )
        poly = (CUBIC_TERM * gram[:, :rows] + QUINTIC_TERM * square_term).astype(jnp.bfloat16)
        product = jnp.einsum("kij,kjl->kil", poly, iterate, preferred_element_type=jnp.float32)
        iterate = (LINEAR_TERM * iterate[:, :rows].astype(jnp.float32) + product).astype(
            jnp.bfloat16
        )
    for group in rounds[ITERS:]:
        for step in group:
            carried = step(carried)
    return iterate, carried


def butterfly_rounds(axis):
    size = lax.axis_size(axis)
    if size & (size - 1):
        return [lambda value: jnp.sum(lax.all_gather(value, axis, axis=0, tiled=False), axis=0)]
    steps = []
    distance = 1
    while distance < size:
        perm = [(i, i ^ distance) for i in range(size)]
        steps.append(lambda value, perm=perm: value + lax.ppermute(value, axis, perm))
        distance *= 2
    return steps


def vector_partials(normed, ln_gain, ln_bias, ln_cotangent, router_cotangent):
    normed_float = normed.astype(jnp.float32)
    cot_float = ln_cotangent.astype(jnp.float32)
    ln_out = (ln_gain[None, :] * normed_float + ln_bias[None, :]).astype(jnp.bfloat16)
    gain_local = jnp.sum(cot_float * normed_float, axis=0)
    bias_local = jnp.sum(cot_float, axis=0)
    router_local = lax.dot_general(
        router_cotangent, ln_out, (((0,), (0,)), ((), ())), preferred_element_type=jnp.float32
    )
    return jnp.concatenate([gain_local[None, :], bias_local[None, :], router_local], axis=0)


def adam(vec_grad, first_moment, second_moment):
    next_first = ADAM_FIRST * first_moment + (1.0 - ADAM_FIRST) * vec_grad
    next_second = ADAM_SECOND * second_moment + (1.0 - ADAM_SECOND) * vec_grad * vec_grad
    adam_step = next_first / (jnp.sqrt(next_second) + ADAM_EPSILON)
    return next_first, next_second, adam_step


def on_device(
    gradient,
    momentum,
    normed,
    ln_gain,
    ln_bias,
    ln_cotangent,
    router_cotangent,
    first_moment,
    second_moment,
):
    grad_float = gradient.astype(jnp.float32)
    next_momentum = MUON_DECAY * momentum + grad_float
    nesterov = (grad_float + MUON_DECAY * next_momentum).astype(jnp.bfloat16)
    count_all, rows_piece, cols_full = nesterov.shape
    inner = lax.axis_size("inner")
    slots = -(-count_all // inner)
    padded = jnp.pad(nesterov, ((0, slots * inner - count_all), (0, 0), (0, 0)))
    by_owner = padded.reshape(inner, slots, rows_piece, cols_full)
    here = lax.axis_index("inner")
    strip = jnp.concatenate(
        [shift(lax.dynamic_index_in_dim(by_owner, (here + k) % inner, 0, keepdims=False), "inner", k)
         for k in range(inner)],
        axis=1,
    )
    blocks = ring_gather(strip, "outer")
    local = vector_partials(normed, ln_gain, ln_bias, ln_cotangent, router_cotangent)
    steps = [step for axis in ("section",) + SHARD for step in butterfly_rounds(axis)]
    rounds = [steps[:2], steps[2:4]] + [[step] for step in steps[4:]]
    result, vec_grad = orthogonalize(blocks, local, rounds, inner * rows_piece)
    next_first, next_second, adam_step = adam(vec_grad, first_moment, second_moment)
    back = jnp.stack(
        [shift(result[:, k * rows_piece:(k + 1) * rows_piece], "inner", -k) for k in range(inner)],
        axis=0,
    )
    twice = jnp.concatenate([back, back], axis=0)
    ordered = lax.dynamic_slice_in_dim(twice, (inner - here) % inner, inner, axis=0)
    ordered = ordered.reshape(inner * slots, rows_piece, cols_full)
    update = ordered[:count_all].astype(jnp.float32) * math.sqrt(FF)
    return (next_momentum, update, next_first, next_second, adam_step)


def inner_size(mesh):
    row = np.asarray(mesh.devices)[:, 0, 0]
    try:
        size = len({tuple(device.coords)[0] for device in row})
    except (AttributeError, TypeError):
        size = 0
    if size <= 1 or row.size % size:
        size = math.gcd(row.size, 4)
    return size


def solution(mesh):
    devices = np.asarray(mesh.devices)
    shard, tensor, section = devices.shape
    inner = inner_size(mesh)
    split = Mesh(
        devices.reshape(shard // inner, inner, tensor, section),
        ("outer", "inner", "tensor", "section"),
    )
    return jax.shard_map(
        on_device,
        mesh=split,
        in_specs=(
            P(("tensor", "section"), SHARD, None),
            P(("tensor", "section"), SHARD, None),
            P((*SHARD, "section"), "tensor"),
            P("tensor"),
            P("tensor"),
            P((*SHARD, "section"), "tensor"),
            P((*SHARD, "section"), None),
            P(None, "tensor"),
            P(None, "tensor"),
        ),
        out_specs=(
            P(("tensor", "section"), SHARD, None),
            P(("tensor", "section"), SHARD, None),
            P(None, "tensor"),
            P(None, "tensor"),
            P(None, "tensor"),
        ),
        check_vma=False,
    )
```

```python
import math

import jax
import jax.numpy as jnp
import numpy as np
from jax import lax
from jax.sharding import Mesh
from jax.sharding import PartitionSpec as P

FF = 2048
ITERS = 5


MUON_DECAY = 0.95
LINEAR_TERM = 3.4445
CUBIC_TERM = -4.775
QUINTIC_TERM = 2.0315
NORM_EPSILON = 1e-07
ADAM_FIRST = 0.9
ADAM_SECOND = 0.95
ADAM_EPSILON = 1e-08

SHARD = ("outer", "inner")


def shift(value, axis, k):
    size = lax.axis_size(axis)
    if k % size == 0:
        return value
    return lax.ppermute(value, axis, [(i, (i + k) % size) for i in range(size)])


def ring_gather(strip, axis):
    size = lax.axis_size(axis)
    cols = strip.shape[-1]
    ahead, behind = [], []
    from_behind = from_ahead = strip
    for distance in range(1, size // 2 + 1):
        if 2 * distance == size:
            half = cols // 2
            first = shift(from_behind[..., :half], axis, 1)
            second = shift(from_ahead[..., half:], axis, -1)
            ahead.append(jnp.concatenate([first, second], axis=-1))
            break
        from_behind = shift(from_behind, axis, 1)
        from_ahead = shift(from_ahead, axis, -1)
        ahead.append(from_ahead)
        behind.append(from_behind)
    return jnp.concatenate([strip] + ahead + behind[::-1], axis=1)


def orthogonalize(blocks, carried, rounds, keep):
    squares = jnp.sum(jnp.square(blocks.astype(jnp.float32)), axis=(1, 2))
    total = jnp.sqrt(squares)
    iterate = (blocks.astype(jnp.float32) / (total + NORM_EPSILON)[:, None, None]).astype(
        jnp.bfloat16
    )
    for repeat in range(ITERS):
        carried, iterate = lax.optimization_barrier((carried, iterate))
        for step in rounds[repeat] if repeat < len(rounds) else ():
            carried = step(carried)
        gram = jnp.einsum("kij,klj->kil", iterate, iterate, preferred_element_type=jnp.float32)
        gram_half = gram.astype(jnp.bfloat16)
        rows = keep if repeat == ITERS - 1 else iterate.shape[1]
        square_term = jnp.einsum(
            "kij,kjl->kil", gram_half[:, :rows], gram_half, preferred_element_type=jnp.float32
        )
        poly = (CUBIC_TERM * gram[:, :rows] + QUINTIC_TERM * square_term).astype(jnp.bfloat16)
        product = jnp.einsum("kij,kjl->kil", poly, iterate, preferred_element_type=jnp.float32)
        iterate = (LINEAR_TERM * iterate[:, :rows].astype(jnp.float32) + product).astype(
            jnp.bfloat16
        )
    for group in rounds[ITERS:]:
        for step in group:
            carried = step(carried)
    return iterate, carried


def butterfly_rounds(axis):
    size = lax.axis_size(axis)
    if size & (size - 1):
        return [lambda value: jnp.sum(lax.all_gather(value, axis, axis=0, tiled=False), axis=0)]
    steps = []
    distance = 1
    while distance < size:
        perm = [(i, i ^ distance) for i in range(size)]
        steps.append(lambda value, perm=perm: value + lax.ppermute(value, axis, perm))
        distance *= 2
    return steps


def vector_partials(normed, ln_gain, ln_bias, ln_cotangent, router_cotangent):
    normed_float = normed.astype(jnp.float32)
    cot_float = ln_cotangent.astype(jnp.float32)
    ln_out = (ln_gain[None, :] * normed_float + ln_bias[None, :]).astype(jnp.bfloat16)
    gain_local = jnp.sum(cot_float * normed_float, axis=0)
    bias_local = jnp.sum(cot_float, axis=0)
    router_local = lax.dot_general(
        router_cotangent, ln_out, (((0,), (0,)), ((), ())), preferred_element_type=jnp.float32
    )
    return jnp.concatenate([gain_local[None, :], bias_local[None, :], router_local], axis=0)


def adam(vec_grad, first_moment, second_moment):
    next_first = ADAM_FIRST * first_moment + (1.0 - ADAM_FIRST) * vec_grad
    next_second = ADAM_SECOND * second_moment + (1.0 - ADAM_SECOND) * vec_grad * vec_grad
    adam_step = next_first / (jnp.sqrt(next_second) + ADAM_EPSILON)
    return next_first, next_second, adam_step


def on_device(
    gradient,
    momentum,
    normed,
    ln_gain,
    ln_bias,
    ln_cotangent,
    router_cotangent,
    first_moment,
    second_moment,
):
    grad_float = gradient.astype(jnp.float32)
    next_momentum = MUON_DECAY * momentum + grad_float
    nesterov = (grad_float + MUON_DECAY * next_momentum).astype(jnp.bfloat16)
    count_all, rows_piece, cols_full = nesterov.shape
    inner = lax.axis_size("inner")
    slots = -(-count_all // inner)
    padded = jnp.pad(nesterov, ((0, slots * inner - count_all), (0, 0), (0, 0)))
    by_owner = padded.reshape(inner, slots, rows_piece, cols_full)
    here = lax.axis_index("inner")
    strip = jnp.concatenate(
        [shift(lax.dynamic_index_in_dim(by_owner, (here + k) % inner, 0, keepdims=False), "inner", k)
         for k in range(inner)],
        axis=1,
    )
    blocks = ring_gather(strip, "outer")
    local = vector_partials(normed, ln_gain, ln_bias, ln_cotangent, router_cotangent)
    steps = [step for axis in SHARD[::-1] + ("section",) for step in butterfly_rounds(axis)]
    rounds = [steps[:2]] + [[step] for step in steps[2:]]
    result, vec_grad = orthogonalize(blocks, local, rounds, inner * rows_piece)
    next_first, next_second, adam_step = adam(vec_grad, first_moment, second_moment)
    back = jnp.stack(
        [shift(result[:, k * rows_piece:(k + 1) * rows_piece], "inner", -k) for k in range(inner)],
        axis=0,
    )
    twice = jnp.concatenate([back, back], axis=0)
    ordered = lax.dynamic_slice_in_dim(twice, (inner - here) % inner, inner, axis=0)
    ordered = ordered.reshape(inner * slots, rows_piece, cols_full)
    update = ordered[:count_all].astype(jnp.float32) * math.sqrt(FF)
    return (next_momentum, update, next_first, next_second, adam_step)


def inner_size(mesh):
    row = np.asarray(mesh.devices)[:, 0, 0]
    try:
        size = len({tuple(device.coords)[0] for device in row})
    except (AttributeError, TypeError):
        size = 0
    if size <= 1 or row.size % size:
        size = math.gcd(row.size, 4)
    return size


def solution(mesh):
    devices = np.asarray(mesh.devices)
    shard, tensor, section = devices.shape
    inner = inner_size(mesh)
    split = Mesh(
        devices.reshape(shard // inner, inner, tensor, section),
        ("outer", "inner", "tensor", "section"),
    )
    return jax.shard_map(
        on_device,
        mesh=split,
        in_specs=(
            P(("tensor", "section"), SHARD, None),
            P(("tensor", "section"), SHARD, None),
            P((*SHARD, "section"), "tensor"),
            P("tensor"),
            P("tensor"),
            P((*SHARD, "section"), "tensor"),
            P((*SHARD, "section"), None),
            P(None, "tensor"),
            P(None, "tensor"),
        ),
        out_specs=(
            P(("tensor", "section"), SHARD, None),
            P(("tensor", "section"), SHARD, None),
            P(None, "tensor"),
            P(None, "tensor"),
            P(None, "tensor"),
        ),
        check_vma=False,
    )
```

```python
import math

import jax
import jax.numpy as jnp
import numpy as np
from jax import lax
from jax.sharding import Mesh
from jax.sharding import PartitionSpec as P

FF = 2048
ITERS = 5


MUON_DECAY = 0.95
LINEAR_TERM = 3.4445
CUBIC_TERM = -4.775
QUINTIC_TERM = 2.0315
NORM_EPSILON = 1e-07
ADAM_FIRST = 0.9
ADAM_SECOND = 0.95
ADAM_EPSILON = 1e-08

SHARD = ("outer", "inner")


def shift(value, axis, k):
    size = lax.axis_size(axis)
    if k % size == 0:
        return value
    return lax.ppermute(value, axis, [(i, (i + k) % size) for i in range(size)])


def ring_gather(strip, axis):
    size = lax.axis_size(axis)
    cols = strip.shape[-1]
    ahead, behind = [], []
    from_behind = from_ahead = strip
    for distance in range(1, size // 2 + 1):
        if 2 * distance == size:
            half = cols // 2
            first = shift(from_behind[..., :half], axis, 1)
            second = shift(from_ahead[..., half:], axis, -1)
            ahead.append(jnp.concatenate([first, second], axis=-1))
            break
        from_behind = shift(from_behind, axis, 1)
        from_ahead = shift(from_ahead, axis, -1)
        ahead.append(from_ahead)
        behind.append(from_behind)
    pieces = [strip] + ahead + behind[::-1]
    squares = sum(jnp.sum(jnp.square(piece.astype(jnp.float32)), axis=(1, 2)) for piece in pieces)
    return jnp.concatenate(pieces, axis=1), squares


def orthogonalize(blocks, squares, carried, rounds, keep):
    total = jnp.sqrt(squares)
    iterate = (blocks.astype(jnp.float32) / (total + NORM_EPSILON)[:, None, None]).astype(
        jnp.bfloat16
    )
    for repeat in range(ITERS):
        carried, iterate = lax.optimization_barrier((carried, iterate))
        for step in rounds[repeat] if repeat < len(rounds) else ():
            carried = step(carried)
        gram = jnp.einsum("kij,klj->kil", iterate, iterate, preferred_element_type=jnp.float32)
        gram_half = gram.astype(jnp.bfloat16)
        rows = keep if repeat == ITERS - 1 else iterate.shape[1]
        square_term = jnp.einsum(
            "kij,kjl->kil", gram_half[:, :rows], gram_half, preferred_element_type=jnp.float32
        )
        poly = (CUBIC_TERM * gram[:, :rows] + QUINTIC_TERM * square_term).astype(jnp.bfloat16)
        product = jnp.einsum("kij,kjl->kil", poly, iterate, preferred_element_type=jnp.float32)
        iterate = (LINEAR_TERM * iterate[:, :rows].astype(jnp.float32) + product).astype(
            jnp.bfloat16
        )
    for group in rounds[ITERS:]:
        for step in group:
            carried = step(carried)
    return iterate, carried


def butterfly_rounds(axis):
    size = lax.axis_size(axis)
    if size & (size - 1):
        return [lambda value: jnp.sum(lax.all_gather(value, axis, axis=0, tiled=False), axis=0)]
    steps = []
    distance = 1
    while distance < size:
        perm = [(i, i ^ distance) for i in range(size)]
        steps.append(lambda value, perm=perm: value + lax.ppermute(value, axis, perm))
        distance *= 2
    return steps


def vector_partials(normed, ln_gain, ln_bias, ln_cotangent, router_cotangent):
    normed_float = normed.astype(jnp.float32)
    cot_float = ln_cotangent.astype(jnp.float32)
    ln_out = (ln_gain[None, :] * normed_float + ln_bias[None, :]).astype(jnp.bfloat16)
    gain_local = jnp.sum(cot_float * normed_float, axis=0)
    bias_local = jnp.sum(cot_float, axis=0)
    router_local = lax.dot_general(
        router_cotangent, ln_out, (((0,), (0,)), ((), ())), preferred_element_type=jnp.float32
    )
    return jnp.concatenate([gain_local[None, :], bias_local[None, :], router_local], axis=0)


def adam(vec_grad, first_moment, second_moment):
    next_first = ADAM_FIRST * first_moment + (1.0 - ADAM_FIRST) * vec_grad
    next_second = ADAM_SECOND * second_moment + (1.0 - ADAM_SECOND) * vec_grad * vec_grad
    adam_step = next_first / (jnp.sqrt(next_second) + ADAM_EPSILON)
    return next_first, next_second, adam_step


def on_device(
    gradient,
    momentum,
    normed,
    ln_gain,
    ln_bias,
    ln_cotangent,
    router_cotangent,
    first_moment,
    second_moment,
):
    grad_float = gradient.astype(jnp.float32)
    next_momentum = MUON_DECAY * momentum + grad_float
    nesterov = (grad_float + MUON_DECAY * next_momentum).astype(jnp.bfloat16)
    count_all, rows_piece, cols_full = nesterov.shape
    inner = lax.axis_size("inner")
    slots = -(-count_all // inner)
    padded = jnp.pad(nesterov, ((0, slots * inner - count_all), (0, 0), (0, 0)))
    by_owner = padded.reshape(inner, slots, rows_piece, cols_full)
    here = lax.axis_index("inner")
    strip = jnp.concatenate(
        [shift(lax.dynamic_index_in_dim(by_owner, (here + k) % inner, 0, keepdims=False), "inner", k)
         for k in range(inner)],
        axis=1,
    )
    blocks, squares = ring_gather(strip, "outer")
    local = vector_partials(normed, ln_gain, ln_bias, ln_cotangent, router_cotangent)
    steps = [step for axis in ("section",) + SHARD for step in butterfly_rounds(axis)]
    rounds = [steps[:2]] + [[step] for step in steps[2:]]
    result, vec_grad = orthogonalize(blocks, squares, local, rounds, inner * rows_piece)
    next_first, next_second, adam_step = adam(vec_grad, first_moment, second_moment)
    back = jnp.stack(
        [shift(result[:, k * rows_piece:(k + 1) * rows_piece], "inner", -k) for k in range(inner)],
        axis=0,
    )
    twice = jnp.concatenate([back, back], axis=0)
    ordered = lax.dynamic_slice_in_dim(twice, (inner - here) % inner, inner, axis=0)
    ordered = ordered.reshape(inner * slots, rows_piece, cols_full)
    update = ordered[:count_all].astype(jnp.float32) * math.sqrt(FF)
    return (next_momentum, update, next_first, next_second, adam_step)


def inner_size(mesh):
    row = np.asarray(mesh.devices)[:, 0, 0]
    try:
        size = len({tuple(device.coords)[0] for device in row})
    except (AttributeError, TypeError):
        size = 0
    if size <= 1 or row.size % size:
        size = math.gcd(row.size, 4)
    return size


def solution(mesh):
    devices = np.asarray(mesh.devices)
    shard, tensor, section = devices.shape
    inner = inner_size(mesh)
    split = Mesh(
        devices.reshape(shard // inner, inner, tensor, section),
        ("outer", "inner", "tensor", "section"),
    )
    return jax.shard_map(
        on_device,
        mesh=split,
        in_specs=(
            P(("tensor", "section"), SHARD, None),
            P(("tensor", "section"), SHARD, None),
            P((*SHARD, "section"), "tensor"),
            P("tensor"),
            P("tensor"),
            P((*SHARD, "section"), "tensor"),
            P((*SHARD, "section"), None),
            P(None, "tensor"),
            P(None, "tensor"),
        ),
        out_specs=(
            P(("tensor", "section"), SHARD, None),
            P(("tensor", "section"), SHARD, None),
            P(None, "tensor"),
            P(None, "tensor"),
            P(None, "tensor"),
        ),
        check_vma=False,
    )
```

```python
import math

import jax
import jax.numpy as jnp
import numpy as np
from jax import lax
from jax.sharding import Mesh
from jax.sharding import PartitionSpec as P

FF = 2048
ITERS = 5


MUON_DECAY = 0.95
LINEAR_TERM = 3.4445
CUBIC_TERM = -4.775
QUINTIC_TERM = 2.0315
NORM_EPSILON = 1e-07
ADAM_FIRST = 0.9
ADAM_SECOND = 0.95
ADAM_EPSILON = 1e-08

SHARD = ("outer", "inner")


def shift(value, axis, k):
    size = lax.axis_size(axis)
    if k % size == 0:
        return value
    return lax.ppermute(value, axis, [(i, (i + k) % size) for i in range(size)])


def ring_gather(strip, axis):
    size = lax.axis_size(axis)
    cols = strip.shape[-1]
    ahead, behind = [], []
    from_behind = from_ahead = strip
    for distance in range(1, size // 2 + 1):
        if 2 * distance == size:
            half = cols // 2
            first = shift(from_behind[..., :half], axis, 1)
            second = shift(from_ahead[..., half:], axis, -1)
            ahead.append(jnp.concatenate([first, second], axis=-1))
            break
        from_behind = shift(from_behind, axis, 1)
        from_ahead = shift(from_ahead, axis, -1)
        ahead.append(from_ahead)
        behind.append(from_behind)
    return jnp.concatenate([strip] + ahead + behind[::-1], axis=1)


def orthogonalize(blocks, carried, rounds, keep):
    squares = jnp.sum(jnp.square(blocks.astype(jnp.float32)), axis=(1, 2))
    total = jnp.sqrt(squares)
    iterate = (blocks.astype(jnp.float32) / (total + NORM_EPSILON)[:, None, None]).astype(
        jnp.bfloat16
    )
    for repeat in range(ITERS):
        carried, iterate = lax.optimization_barrier((carried, iterate))
        for step in rounds[repeat] if repeat < len(rounds) else ():
            carried = step(carried)
        gram = jnp.einsum("kij,klj->kil", iterate, iterate, preferred_element_type=jnp.float32)
        gram_half = gram.astype(jnp.bfloat16)
        rows = keep if repeat == ITERS - 1 else iterate.shape[1]
        square_term = jnp.einsum(
            "kij,kjl->kil", gram_half[:, :rows], gram_half, preferred_element_type=jnp.float32
        )
        poly = (CUBIC_TERM * gram[:, :rows] + QUINTIC_TERM * square_term).astype(jnp.bfloat16)
        product = jnp.einsum("kij,kjl->kil", poly, iterate, preferred_element_type=jnp.float32)
        iterate = (LINEAR_TERM * iterate[:, :rows].astype(jnp.float32) + product).astype(
            jnp.bfloat16
        )
    for group in rounds[ITERS:]:
        for step in group:
            carried = step(carried)
    return iterate, carried


def butterfly_rounds(axis):
    size = lax.axis_size(axis)
    if size & (size - 1):
        return [lambda value: jnp.sum(lax.all_gather(value, axis, axis=0, tiled=False), axis=0)]
    steps = []
    distance = 1
    while distance < size:
        perm = [(i, i ^ distance) for i in range(size)]
        steps.append(lambda value, perm=perm: value + lax.ppermute(value, axis, perm))
        distance *= 2
    return steps


def vector_partials(normed, ln_gain, ln_bias, ln_cotangent, router_cotangent):
    normed_float = normed.astype(jnp.float32)
    cot_float = ln_cotangent.astype(jnp.float32)
    ln_out = (ln_gain[None, :] * normed_float + ln_bias[None, :]).astype(jnp.bfloat16)
    gain_local = jnp.sum(cot_float * normed_float, axis=0)
    bias_local = jnp.sum(cot_float, axis=0)
    router_local = lax.dot_general(
        router_cotangent, ln_out, (((0,), (0,)), ((), ())), preferred_element_type=jnp.float32
    )
    return jnp.concatenate([gain_local[None, :], bias_local[None, :], router_local], axis=0)


def adam(vec_grad, first_moment, second_moment):
    next_first = ADAM_FIRST * first_moment + (1.0 - ADAM_FIRST) * vec_grad
    next_second = ADAM_SECOND * second_moment + (1.0 - ADAM_SECOND) * vec_grad * vec_grad
    adam_step = next_first / (jnp.sqrt(next_second) + ADAM_EPSILON)
    return next_first, next_second, adam_step


def on_device(
    gradient,
    momentum,
    normed,
    ln_gain,
    ln_bias,
    ln_cotangent,
    router_cotangent,
    first_moment,
    second_moment,
):
    grad_float = gradient.astype(jnp.float32)
    nesterov = (grad_float + MUON_DECAY * (MUON_DECAY * momentum + grad_float)).astype(jnp.bfloat16)
    count_all, rows_piece, cols_full = nesterov.shape
    inner = lax.axis_size("inner")
    slots = -(-count_all // inner)
    padded = jnp.pad(nesterov, ((0, slots * inner - count_all), (0, 0), (0, 0)))
    by_owner = padded.reshape(inner, slots, rows_piece, cols_full)
    here = lax.axis_index("inner")
    strip = jnp.concatenate(
        [shift(lax.dynamic_index_in_dim(by_owner, (here + k) % inner, 0, keepdims=False), "inner", k)
         for k in range(inner)],
        axis=1,
    )
    momentum, grad_float, strip = lax.optimization_barrier((momentum, grad_float, strip))
    next_momentum = MUON_DECAY * momentum + grad_float
    blocks = ring_gather(strip, "outer")
    local = vector_partials(normed, ln_gain, ln_bias, ln_cotangent, router_cotangent)
    steps = [step for axis in ("section",) + SHARD for step in butterfly_rounds(axis)]
    rounds = [steps[:2]] + [[step] for step in steps[2:]]
    result, vec_grad = orthogonalize(blocks, local, rounds, inner * rows_piece)
    next_first, next_second, adam_step = adam(vec_grad, first_moment, second_moment)
    back = jnp.stack(
        [shift(result[:, k * rows_piece:(k + 1) * rows_piece], "inner", -k) for k in range(inner)],
        axis=0,
    )
    twice = jnp.concatenate([back, back], axis=0)
    ordered = lax.dynamic_slice_in_dim(twice, (inner - here) % inner, inner, axis=0)
    ordered = ordered.reshape(inner * slots, rows_piece, cols_full)
    update = ordered[:count_all].astype(jnp.float32) * math.sqrt(FF)
    return (next_momentum, update, next_first, next_second, adam_step)


def inner_size(mesh):
    row = np.asarray(mesh.devices)[:, 0, 0]
    try:
        size = len({tuple(device.coords)[0] for device in row})
    except (AttributeError, TypeError):
        size = 0
    if size <= 1 or row.size % size:
        size = math.gcd(row.size, 4)
    return size


def solution(mesh):
    devices = np.asarray(mesh.devices)
    shard, tensor, section = devices.shape
    inner = inner_size(mesh)
    split = Mesh(
        devices.reshape(shard // inner, inner, tensor, section),
        ("outer", "inner", "tensor", "section"),
    )
    return jax.shard_map(
        on_device,
        mesh=split,
        in_specs=(
            P(("tensor", "section"), SHARD, None),
            P(("tensor", "section"), SHARD, None),
            P((*SHARD, "section"), "tensor"),
            P("tensor"),
            P("tensor"),
            P((*SHARD, "section"), "tensor"),
            P((*SHARD, "section"), None),
            P(None, "tensor"),
            P(None, "tensor"),
        ),
        out_specs=(
            P(("tensor", "section"), SHARD, None),
            P(("tensor", "section"), SHARD, None),
            P(None, "tensor"),
            P(None, "tensor"),
            P(None, "tensor"),
        ),
        check_vma=False,
    )
```

```python
import math

import jax
import jax.numpy as jnp
import numpy as np
from jax import lax
from jax.sharding import Mesh
from jax.sharding import PartitionSpec as P

FF = 2048
ITERS = 5


MUON_DECAY = 0.95
LINEAR_TERM = 3.4445
CUBIC_TERM = -4.775
QUINTIC_TERM = 2.0315
NORM_EPSILON = 1e-07
ADAM_FIRST = 0.9
ADAM_SECOND = 0.95
ADAM_EPSILON = 1e-08

SHARD = ("outer", "inner")


def shift(value, axis, k):
    size = lax.axis_size(axis)
    if k % size == 0:
        return value
    return lax.ppermute(value, axis, [(i, (i + k) % size) for i in range(size)])


def ring_gather(strip, axis):
    size = lax.axis_size(axis)
    cols = strip.shape[-1]
    ahead, behind = [], []
    from_behind = from_ahead = strip
    for distance in range(1, size // 2 + 1):
        if 2 * distance == size:
            half = cols // 2
            first = shift(from_behind[..., :half], axis, 1)
            second = shift(from_ahead[..., half:], axis, -1)
            ahead.append(jnp.concatenate([first, second], axis=-1))
            break
        from_behind = shift(from_behind, axis, 1)
        from_ahead = shift(from_ahead, axis, -1)
        ahead.append(from_ahead)
        behind.append(from_behind)
    return jnp.concatenate([strip] + ahead + behind[::-1], axis=1)


def orthogonalize(blocks, carried, rounds, keep):
    squares = jnp.sum(jnp.square(blocks.astype(jnp.float32)), axis=(1, 2))
    total = jnp.sqrt(squares)
    iterate = (blocks.astype(jnp.float32) / (total + NORM_EPSILON)[:, None, None]).astype(
        jnp.bfloat16
    )
    for repeat in range(ITERS):
        carried, iterate = lax.optimization_barrier((carried, iterate))
        for step in rounds[repeat] if repeat < len(rounds) else ():
            carried = step(carried)
        gram = jnp.einsum("kij,klj->kil", iterate, iterate, preferred_element_type=jnp.float32)
        gram_half = gram.astype(jnp.bfloat16)
        rows = keep if repeat == ITERS - 1 else iterate.shape[1]
        square_term = jnp.einsum(
            "kij,kjl->kil", gram_half[:, :rows], gram_half, preferred_element_type=jnp.float32
        )
        poly = (CUBIC_TERM * gram[:, :rows] + QUINTIC_TERM * square_term).astype(jnp.bfloat16)
        if repeat == ITERS - 1:
            carried, poly = lax.optimization_barrier((carried, poly))
        product = jnp.einsum("kij,kjl->kil", poly, iterate, preferred_element_type=jnp.float32)
        iterate = (LINEAR_TERM * iterate[:, :rows].astype(jnp.float32) + product).astype(
            jnp.bfloat16
        )
    for group in rounds[ITERS:]:
        for step in group:
            carried = step(carried)
    return iterate, carried


def butterfly_rounds(axis):
    size = lax.axis_size(axis)
    if size & (size - 1):
        return [lambda value: jnp.sum(lax.all_gather(value, axis, axis=0, tiled=False), axis=0)]
    steps = []
    distance = 1
    while distance < size:
        perm = [(i, i ^ distance) for i in range(size)]
        steps.append(lambda value, perm=perm: value + lax.ppermute(value, axis, perm))
        distance *= 2
    return steps


def vector_partials(normed, ln_gain, ln_bias, ln_cotangent, router_cotangent):
    normed_float = normed.astype(jnp.float32)
    cot_float = ln_cotangent.astype(jnp.float32)
    ln_out = (ln_gain[None, :] * normed_float + ln_bias[None, :]).astype(jnp.bfloat16)
    gain_local = jnp.sum(cot_float * normed_float, axis=0)
    bias_local = jnp.sum(cot_float, axis=0)
    router_local = lax.dot_general(
        router_cotangent, ln_out, (((0,), (0,)), ((), ())), preferred_element_type=jnp.float32
    )
    return jnp.concatenate([gain_local[None, :], bias_local[None, :], router_local], axis=0)


def adam(vec_grad, first_moment, second_moment):
    next_first = ADAM_FIRST * first_moment + (1.0 - ADAM_FIRST) * vec_grad
    next_second = ADAM_SECOND * second_moment + (1.0 - ADAM_SECOND) * vec_grad * vec_grad
    adam_step = next_first / (jnp.sqrt(next_second) + ADAM_EPSILON)
    return next_first, next_second, adam_step


def on_device(
    gradient,
    momentum,
    normed,
    ln_gain,
    ln_bias,
    ln_cotangent,
    router_cotangent,
    first_moment,
    second_moment,
):
    grad_float = gradient.astype(jnp.float32)
    next_momentum = MUON_DECAY * momentum + grad_float
    nesterov = (grad_float + MUON_DECAY * next_momentum).astype(jnp.bfloat16)
    count_all, rows_piece, cols_full = nesterov.shape
    inner = lax.axis_size("inner")
    slots = -(-count_all // inner)
    padded = jnp.pad(nesterov, ((0, slots * inner - count_all), (0, 0), (0, 0)))
    by_owner = padded.reshape(inner, slots, rows_piece, cols_full)
    here = lax.axis_index("inner")
    strip = jnp.concatenate(
        [shift(lax.dynamic_index_in_dim(by_owner, (here + k) % inner, 0, keepdims=False), "inner", k)
         for k in range(inner)],
        axis=1,
    )
    blocks = ring_gather(strip, "outer")
    local = vector_partials(normed, ln_gain, ln_bias, ln_cotangent, router_cotangent)
    steps = [step for axis in ("section",) + SHARD for step in butterfly_rounds(axis)]
    rounds = [steps[:2]] + [[step] for step in steps[2:]]
    result, vec_grad = orthogonalize(blocks, local, rounds, inner * rows_piece)
    next_first, next_second, adam_step = adam(vec_grad, first_moment, second_moment)
    back = jnp.stack(
        [shift(result[:, k * rows_piece:(k + 1) * rows_piece], "inner", -k) for k in range(inner)],
        axis=0,
    )
    twice = jnp.concatenate([back, back], axis=0)
    ordered = lax.dynamic_slice_in_dim(twice, (inner - here) % inner, inner, axis=0)
    ordered = ordered.reshape(inner * slots, rows_piece, cols_full)
    update = ordered[:count_all].astype(jnp.float32) * math.sqrt(FF)
    return (next_momentum, update, next_first, next_second, adam_step)


def inner_size(mesh):
    row = np.asarray(mesh.devices)[:, 0, 0]
    try:
        size = len({tuple(device.coords)[0] for device in row})
    except (AttributeError, TypeError):
        size = 0
    if size <= 1 or row.size % size:
        size = math.gcd(row.size, 4)
    return size


def solution(mesh):
    devices = np.asarray(mesh.devices)
    shard, tensor, section = devices.shape
    inner = inner_size(mesh)
    split = Mesh(
        devices.reshape(shard // inner, inner, tensor, section),
        ("outer", "inner", "tensor", "section"),
    )
    return jax.shard_map(
        on_device,
        mesh=split,
        in_specs=(
            P(("tensor", "section"), SHARD, None),
            P(("tensor", "section"), SHARD, None),
            P((*SHARD, "section"), "tensor"),
            P("tensor"),
            P("tensor"),
            P((*SHARD, "section"), "tensor"),
            P((*SHARD, "section"), None),
            P(None, "tensor"),
            P(None, "tensor"),
        ),
        out_specs=(
            P(("tensor", "section"), SHARD, None),
            P(("tensor", "section"), SHARD, None),
            P(None, "tensor"),
            P(None, "tensor"),
            P(None, "tensor"),
        ),
        check_vma=False,
    )
```

```python
import math

import jax
import jax.numpy as jnp
import numpy as np
from jax import lax
from jax.sharding import Mesh
from jax.sharding import PartitionSpec as P

FF = 2048
ITERS = 5


MUON_DECAY = 0.95
LINEAR_TERM = 3.4445
CUBIC_TERM = -4.775
QUINTIC_TERM = 2.0315
NORM_EPSILON = 1e-07
ADAM_FIRST = 0.9
ADAM_SECOND = 0.95
ADAM_EPSILON = 1e-08

SHARD = ("outer", "inner")


def shift(value, axis, k):
    size = lax.axis_size(axis)
    if k % size == 0:
        return value
    return lax.ppermute(value, axis, [(i, (i + k) % size) for i in range(size)])


def ring_gather(strip, axis):
    size = lax.axis_size(axis)
    cols = strip.shape[-1]
    ahead, behind = [], []
    from_behind = from_ahead = strip
    for distance in range(1, size // 2 + 1):
        if 2 * distance == size:
            half = cols // 2
            first = shift(from_behind[..., :half], axis, 1)
            second = shift(from_ahead[..., half:], axis, -1)
            ahead.append(jnp.concatenate([first, second], axis=-1))
            break
        from_behind = shift(from_behind, axis, 1)
        from_ahead = shift(from_ahead, axis, -1)
        ahead.append(from_ahead)
        behind.append(from_behind)
    return jnp.concatenate([strip] + ahead + behind[::-1], axis=1)


def orthogonalize(blocks, carried, rounds, keep):
    squares = jnp.sum(jnp.square(blocks.astype(jnp.float32)), axis=(1, 2))
    total = jnp.sqrt(squares)
    iterate = (blocks.astype(jnp.float32) / (total + NORM_EPSILON)[:, None, None]).astype(
        jnp.bfloat16
    )
    for repeat in range(ITERS):
        carried, iterate = lax.optimization_barrier((carried, iterate))
        for step in rounds[repeat] if repeat < len(rounds) else ():
            carried = step(carried)
        gram = jnp.einsum("kij,klj->kil", iterate, iterate, preferred_element_type=jnp.float32)
        gram_half = gram.astype(jnp.bfloat16)
        rows = keep if repeat == ITERS - 1 else iterate.shape[1]
        square_term = jnp.einsum(
            "kij,kjl->kil", gram_half[:, :rows], gram_half, preferred_element_type=jnp.float32
        )
        poly = (CUBIC_TERM * gram[:, :rows] + QUINTIC_TERM * square_term).astype(jnp.bfloat16)
        product = jnp.einsum("kij,kjl->kil", poly, iterate, preferred_element_type=jnp.float32)
        iterate = (LINEAR_TERM * iterate[:, :rows].astype(jnp.float32) + product).astype(
            jnp.bfloat16
        )
    for group in rounds[ITERS:]:
        for step in group:
            carried = step(carried)
    return iterate, carried


def butterfly_rounds(axis):
    size = lax.axis_size(axis)
    if size & (size - 1):
        return [lambda value: jnp.sum(lax.all_gather(value, axis, axis=0, tiled=False), axis=0)]
    steps = []
    distance = 1
    while distance < size:
        perm = [(i, i ^ distance) for i in range(size)]
        steps.append(lambda value, perm=perm: value + lax.ppermute(value, axis, perm))
        distance *= 2
    return steps


def vector_partials(normed, ln_gain, ln_bias, ln_cotangent, router_cotangent):
    normed_float = normed.astype(jnp.float32)
    cot_float = ln_cotangent.astype(jnp.float32)
    ln_out = (ln_gain[None, :] * normed_float + ln_bias[None, :]).astype(jnp.bfloat16)
    gain_local = jnp.sum(cot_float * normed_float, axis=0)
    bias_local = jnp.sum(cot_float, axis=0)
    router_local = lax.dot_general(
        router_cotangent, ln_out, (((0,), (0,)), ((), ())), preferred_element_type=jnp.float32
    )
    return jnp.concatenate([gain_local[None, :], bias_local[None, :], router_local], axis=0)


def adam(vec_grad, first_moment, second_moment):
    next_first = ADAM_FIRST * first_moment + (1.0 - ADAM_FIRST) * vec_grad
    next_second = ADAM_SECOND * second_moment + (1.0 - ADAM_SECOND) * vec_grad * vec_grad
    adam_step = next_first / (jnp.sqrt(next_second) + ADAM_EPSILON)
    return next_first, next_second, adam_step


def on_device(
    gradient,
    momentum,
    normed,
    ln_gain,
    ln_bias,
    ln_cotangent,
    router_cotangent,
    first_moment,
    second_moment,
):
    grad_float = gradient.astype(jnp.float32)
    next_momentum = MUON_DECAY * momentum + grad_float
    nesterov = (grad_float + MUON_DECAY * next_momentum).astype(jnp.bfloat16)
    count_all, rows_piece, cols_full = nesterov.shape
    inner = lax.axis_size("inner")
    slots = -(-count_all // inner)
    padded = jnp.pad(nesterov, ((0, slots * inner - count_all), (0, 0), (0, 0)))
    by_owner = padded.reshape(inner, slots, rows_piece, cols_full)
    here = lax.axis_index("inner")
    strip = jnp.concatenate(
        [shift(lax.dynamic_index_in_dim(by_owner, (here + k) % inner, 0, keepdims=False), "inner", k)
         for k in range(inner)],
        axis=1,
    )
    blocks = ring_gather(strip, "outer")
    local = vector_partials(normed, ln_gain, ln_bias, ln_cotangent, router_cotangent)
    steps = [step for axis in ("section",) + SHARD for step in butterfly_rounds(axis)]
    rounds = [steps[:2]] + [[step] for step in steps[2:]]
    result, vec_grad = orthogonalize(blocks, local, rounds, inner * rows_piece)
    next_first, next_second, adam_step = adam(vec_grad, first_moment, second_moment)
    back = jnp.stack(
        [shift(result[:, k * rows_piece:(k + 1) * rows_piece], "inner", -k) for k in range(inner)],
        axis=0,
    )
    ordered = jnp.take(back, (jnp.arange(inner) - here) % inner, axis=0)
    ordered = ordered.reshape(inner * slots, rows_piece, cols_full)
    update = ordered[:count_all].astype(jnp.float32) * math.sqrt(FF)
    return (next_momentum, update, next_first, next_second, adam_step)


def inner_size(mesh):
    row = np.asarray(mesh.devices)[:, 0, 0]
    try:
        size = len({tuple(device.coords)[0] for device in row})
    except (AttributeError, TypeError):
        size = 0
    if size <= 1 or row.size % size:
        size = math.gcd(row.size, 4)
    return size


def solution(mesh):
    devices = np.asarray(mesh.devices)
    shard, tensor, section = devices.shape
    inner = inner_size(mesh)
    split = Mesh(
        devices.reshape(shard // inner, inner, tensor, section),
        ("outer", "inner", "tensor", "section"),
    )
    return jax.shard_map(
        on_device,
        mesh=split,
        in_specs=(
            P(("tensor", "section"), SHARD, None),
            P(("tensor", "section"), SHARD, None),
            P((*SHARD, "section"), "tensor"),
            P("tensor"),
            P("tensor"),
            P((*SHARD, "section"), "tensor"),
            P((*SHARD, "section"), None),
            P(None, "tensor"),
            P(None, "tensor"),
        ),
        out_specs=(
            P(("tensor", "section"), SHARD, None),
            P(("tensor", "section"), SHARD, None),
            P(None, "tensor"),
            P(None, "tensor"),
            P(None, "tensor"),
        ),
        check_vma=False,
    )
```

```python
import math

import jax
import jax.numpy as jnp
import numpy as np
from jax import lax
from jax.sharding import Mesh
from jax.sharding import PartitionSpec as P

FF = 2048
ITERS = 5


MUON_DECAY = 0.95
LINEAR_TERM = 3.4445
CUBIC_TERM = -4.775
QUINTIC_TERM = 2.0315
NORM_EPSILON = 1e-07
ADAM_FIRST = 0.9
ADAM_SECOND = 0.95
ADAM_EPSILON = 1e-08

SHARD = ("outer", "inner")


def shift(value, axis, k):
    size = lax.axis_size(axis)
    if k % size == 0:
        return value
    return lax.ppermute(value, axis, [(i, (i + k) % size) for i in range(size)])


def ring_gather(strip, axis):
    size = lax.axis_size(axis)
    cols = strip.shape[-1]
    ahead, behind = [], []
    far = []
    if size % 2 == 0 and size > 2:
        half = cols // 2
        far = [jnp.concatenate(
            [shift(strip[..., :half], axis, size // 2), shift(strip[..., half:], axis, -(size // 2))],
            axis=-1)]
    from_behind = from_ahead = strip
    for distance in range(1, (size + 1) // 2):
        from_behind = shift(from_behind, axis, 1)
        from_ahead = shift(from_ahead, axis, -1)
        ahead.append(from_ahead)
        behind.append(from_behind)
    if size == 2:
        far = [shift(strip, axis, 1)]
    return jnp.concatenate([strip] + ahead + far + behind[::-1], axis=1)


def orthogonalize(blocks, carried, rounds, keep):
    squares = jnp.sum(jnp.square(blocks.astype(jnp.float32)), axis=(1, 2))
    total = jnp.sqrt(squares)
    iterate = (blocks.astype(jnp.float32) / (total + NORM_EPSILON)[:, None, None]).astype(
        jnp.bfloat16
    )
    for repeat in range(ITERS):
        carried, iterate = lax.optimization_barrier((carried, iterate))
        for step in rounds[repeat] if repeat < len(rounds) else ():
            carried = step(carried)
        gram = jnp.einsum("kij,klj->kil", iterate, iterate, preferred_element_type=jnp.float32)
        gram_half = gram.astype(jnp.bfloat16)
        rows = keep if repeat == ITERS - 1 else iterate.shape[1]
        square_term = jnp.einsum(
            "kij,kjl->kil", gram_half[:, :rows], gram_half, preferred_element_type=jnp.float32
        )
        poly = (CUBIC_TERM * gram[:, :rows] + QUINTIC_TERM * square_term).astype(jnp.bfloat16)
        product = jnp.einsum("kij,kjl->kil", poly, iterate, preferred_element_type=jnp.float32)
        iterate = (LINEAR_TERM * iterate[:, :rows].astype(jnp.float32) + product).astype(
            jnp.bfloat16
        )
    for group in rounds[ITERS:]:
        for step in group:
            carried = step(carried)
    return iterate, carried


def butterfly_rounds(axis):
    size = lax.axis_size(axis)
    if size & (size - 1):
        return [lambda value: jnp.sum(lax.all_gather(value, axis, axis=0, tiled=False), axis=0)]
    steps = []
    distance = 1
    while distance < size:
        perm = [(i, i ^ distance) for i in range(size)]
        steps.append(lambda value, perm=perm: value + lax.ppermute(value, axis, perm))
        distance *= 2
    return steps


def vector_partials(normed, ln_gain, ln_bias, ln_cotangent, router_cotangent):
    normed_float = normed.astype(jnp.float32)
    cot_float = ln_cotangent.astype(jnp.float32)
    ln_out = (ln_gain[None, :] * normed_float + ln_bias[None, :]).astype(jnp.bfloat16)
    gain_local = jnp.sum(cot_float * normed_float, axis=0)
    bias_local = jnp.sum(cot_float, axis=0)
    router_local = lax.dot_general(
        router_cotangent, ln_out, (((0,), (0,)), ((), ())), preferred_element_type=jnp.float32
    )
    return jnp.concatenate([gain_local[None, :], bias_local[None, :], router_local], axis=0)


def adam(vec_grad, first_moment, second_moment):
    next_first = ADAM_FIRST * first_moment + (1.0 - ADAM_FIRST) * vec_grad
    next_second = ADAM_SECOND * second_moment + (1.0 - ADAM_SECOND) * vec_grad * vec_grad
    adam_step = next_first / (jnp.sqrt(next_second) + ADAM_EPSILON)
    return next_first, next_second, adam_step


def on_device(
    gradient,
    momentum,
    normed,
    ln_gain,
    ln_bias,
    ln_cotangent,
    router_cotangent,
    first_moment,
    second_moment,
):
    grad_float = gradient.astype(jnp.float32)
    next_momentum = MUON_DECAY * momentum + grad_float
    nesterov = (grad_float + MUON_DECAY * next_momentum).astype(jnp.bfloat16)
    count_all, rows_piece, cols_full = nesterov.shape
    inner = lax.axis_size("inner")
    slots = -(-count_all // inner)
    padded = jnp.pad(nesterov, ((0, slots * inner - count_all), (0, 0), (0, 0)))
    by_owner = padded.reshape(inner, slots, rows_piece, cols_full)
    here = lax.axis_index("inner")
    strip = jnp.concatenate(
        [shift(lax.dynamic_index_in_dim(by_owner, (here + k) % inner, 0, keepdims=False), "inner", k)
         for k in range(inner)],
        axis=1,
    )
    blocks = ring_gather(strip, "outer")
    local = vector_partials(normed, ln_gain, ln_bias, ln_cotangent, router_cotangent)
    steps = [step for axis in ("section",) + SHARD for step in butterfly_rounds(axis)]
    rounds = [steps[:2]] + [[step] for step in steps[2:]]
    result, vec_grad = orthogonalize(blocks, local, rounds, inner * rows_piece)
    next_first, next_second, adam_step = adam(vec_grad, first_moment, second_moment)
    back = jnp.stack(
        [shift(result[:, k * rows_piece:(k + 1) * rows_piece], "inner", -k) for k in range(inner)],
        axis=0,
    )
    twice = jnp.concatenate([back, back], axis=0)
    ordered = lax.dynamic_slice_in_dim(twice, (inner - here) % inner, inner, axis=0)
    ordered = ordered.reshape(inner * slots, rows_piece, cols_full)
    update = ordered[:count_all].astype(jnp.float32) * math.sqrt(FF)
    return (next_momentum, update, next_first, next_second, adam_step)


def inner_size(mesh):
    row = np.asarray(mesh.devices)[:, 0, 0]
    try:
        size = len({tuple(device.coords)[0] for device in row})
    except (AttributeError, TypeError):
        size = 0
    if size <= 1 or row.size % size:
        size = math.gcd(row.size, 4)
    return size


def solution(mesh):
    devices = np.asarray(mesh.devices)
    shard, tensor, section = devices.shape
    inner = inner_size(mesh)
    split = Mesh(
        devices.reshape(shard // inner, inner, tensor, section),
        ("outer", "inner", "tensor", "section"),
    )
    return jax.shard_map(
        on_device,
        mesh=split,
        in_specs=(
            P(("tensor", "section"), SHARD, None),
            P(("tensor", "section"), SHARD, None),
            P((*SHARD, "section"), "tensor"),
            P("tensor"),
            P("tensor"),
            P((*SHARD, "section"), "tensor"),
            P((*SHARD, "section"), None),
            P(None, "tensor"),
            P(None, "tensor"),
        ),
        out_specs=(
            P(("tensor", "section"), SHARD, None),
            P(("tensor", "section"), SHARD, None),
            P(None, "tensor"),
            P(None, "tensor"),
            P(None, "tensor"),
        ),
        check_vma=False,
    )
```
